32 devices in a mesh: tm: 8 (over z, y), cal: 4 (over x, core).
Axes of the slice: x: 2, y: 2, z: 4, core: 2. Of those that a mesh axis runs over, the one named last changes fastest.
Arguments:
- src_design: float32 [5, 4096, 128], P(None, ('tm', 'cal')), may hold values from -6 to 6
- att_design: float32 [3, 4096, 128], P(None, ('tm', 'cal')), may hold values from -6 to 6
- obs_phase: float32 [4096, 128], P(('tm', 'cal')), may hold values from 0 to 1
- cal_design: float32 [4096, 128], P(('tm', 'cal')), may hold values from -6 to 6
- obs_weight: float32 [4096, 128], P(('tm', 'cal')), may hold values from 0.1 to 12
- knot_index: int32 [4096, 128], P(('tm', 'cal')), may hold values from 0 to 4092, as said below
- cal_block: int32 [4096, 128], P(('tm', 'cal')), may hold values from 0 to 7
- cal_column: int32 [4096, 128], P(('tm', 'cal')), may hold values from 0 to 4095
- obs_count: int32 [4096], P(('tm', 'cal')), may hold values from 32 to 128
- src_res: float32 [5, 4096], P(None, ('tm', 'cal')), may hold values from -6 to 6
- att_res: float32 [3, 4096], P(None, ('tm', 'cal')), may hold values from -6 to 6
- cal_res: float32 [8, 4096], P('cal'), may hold values from -6 to 6
- src_dir: float32 [5, 4096], P(None, ('tm', 'cal')), may hold values from -6 to 6
- att_dir: float32 [3, 4096], P(None, ('tm', 'cal')), may hold values from -6 to 6
- cal_dir: float32 [8, 4096], P('cal'), may hold values from -6 to 6
Outputs:
- new_src_res: float32 [5, 4096], P(None, ('tm', 'cal'))
- new_att_res: float32 [3, 4096], P(None, ('tm', 'cal'))
- new_cal_res: float32 [8, 4096], P('cal')
- new_src_dir: float32 [5, 4096], P(None, ('tm', 'cal'))
- new_att_dir: float32 [3, 4096], P(None, ('tm', 'cal'))
- new_cal_dir: float32 [8, 4096], P('cal')
The draws below stay inside these ranges and needn't reach their ends.
Inputs may be any that keep to these rules, and one draw needn't show every extreme that they name: The observations of source row s have knot intervals from (s // 128) * 128 to (s // 128) * 128 + 127, and knot_index + 3 < 4096.
All inputs are finite; a program needn't handle non-finite values.
Results may differ from the reference program's by a relative error of at most 0.00015.
Values sent between devices are 32-bit elements; how exact they have to be, the bound alone decides.
No kernel may reach another device: no remote copies, remote signals or barrier semaphores. Data moves between devices by JAX's collectives and lax.ppermute only.
A program may use at most 64 MiB of HBM per device.

```python
import math
import jax
import jax.numpy as jnp

NOBS = 128
CW = 4096
SRC_DEV = 128
KNOT_DEV = 128
NCB = 8
NSRC = 4096
NKNOT = 4096


def draw_knot_index(key, part):
    segment = jnp.arange(NSRC, dtype=jnp.int32)[:, None] // SRC_DEV
    final_dev = NSRC // SRC_DEV - 1
    upper = jnp.where(segment == final_dev, KNOT_DEV - 3, KNOT_DEV)
    upper = jnp.broadcast_to(upper, (NSRC, NOBS))
    local = jax.random.randint(key, (NSRC, NOBS), 0, upper)
    return (segment * KNOT_DEV + local).astype(jnp.int32)


def draw_obs_weight(key, part):
    position = jnp.arange(NSRC, dtype=jnp.float32)[:, None] / NSRC
    spread = jnp.exp(jax.random.uniform(key, (NSRC, NOBS), jnp.float32, math.log(0.2), math.log(2.0)))
    return spread * (1.0 + 2.0 * position)


def place_ends(entries, rng, low, largest):
    shape = entries.shape
    place = [jax.random.randint(jax.random.fold_in(rng, axis), (), 0, shape[axis]) for axis in range(len(shape))]
    entries = entries.at[tuple(place)].set(low)
    longest = shape.index(max(shape))
    place[longest] = (place[longest] + 1) % shape[longest]
    return entries.at[tuple(place)].set(largest)


def steps_of(key, shape, shards, low, high):
    level, own = 1.0, jax.random.fold_in(key, 6)
    for axis_at, parts in shards:
        draws = jnp.exp(jax.random.uniform(jax.random.fold_in(own, axis_at), (parts,), jnp.float32, low / len(shards), high / len(shards)))
        level = level * jnp.repeat(draws, shape[axis_at] // parts).reshape([-1 if axis == axis_at else 1 for axis in range(len(shape))])
    return level


def centred(key, dims, scale, bound, shards=(), held_as=jnp.bfloat16):
    array = scale * jax.random.normal(key, dims, jnp.float32)
    if shards:
        array = array * steps_of(key, dims, shards, -0.22, 0.18)
    return jnp.clip(array, -bound, bound).astype(held_as)


def setup_inputs(seed: int = 0) -> dict:
    streams_of = jax.random.split(jax.random.key(seed), 16)
    src_design = centred(streams_of[0], (5, NSRC, NOBS), 1.0, 6.0, ((1, 32),), jnp.float32)
    att_design = centred(streams_of[1], (3, NSRC, NOBS), 1.0, 6.0, ((1, 32),), jnp.float32)
    obs_phase = jnp.clip(1.0 * jax.random.uniform(streams_of[2], (NSRC, NOBS), jnp.float32) ** steps_of(streams_of[2], (NSRC, NOBS), ((0, 32),), -0.2, 0.2), 0.0, 1.0)
    cal_design = centred(streams_of[3], (NSRC, NOBS), 1.0, 6.0, ((0, 32),), jnp.float32)
    obs_weight = draw_obs_weight(jax.random.fold_in(streams_of[15], 71), 0)
    knot_index = draw_knot_index(jax.random.fold_in(streams_of[15], 71), 0)
    cal_block = place_ends(jax.random.randint(streams_of[6], (NSRC, NOBS), 0, NCB), jax.random.fold_in(streams_of[6], 1), 0, NCB - 1).astype(jnp.int32)
    cal_column = place_ends(jax.random.randint(streams_of[7], (NSRC, NOBS), 0, CW), jax.random.fold_in(streams_of[7], 1), 0, CW - 1).astype(jnp.int32)
    obs_count = place_ends(jax.random.randint(streams_of[8], (NSRC,), 32, NOBS + 1), jax.random.fold_in(streams_of[8], 1), 32, NOBS).astype(jnp.int32)
    src_res = centred(streams_of[9], (5, NSRC), 1.0, 6.0, ((1, 32),), jnp.float32)
    att_res = centred(streams_of[10], (3, NKNOT), 1.0, 6.0, ((1, 32),), jnp.float32)
    cal_res = centred(streams_of[11], (NCB, CW), 1.0, 6.0, ((0, 4),), jnp.float32)
    src_dir = centred(streams_of[12], (5, NSRC), 1.0, 6.0, ((1, 32),), jnp.float32)
    att_dir = centred(streams_of[13], (3, NKNOT), 1.0, 6.0, ((1, 32),), jnp.float32)
    cal_dir = centred(streams_of[14], (NCB, CW), 1.0, 6.0, ((0, 4),), jnp.float32)
    return {"src_design": src_design, "att_design": att_design, "obs_phase": obs_phase, "cal_design": cal_design, "obs_weight": obs_weight, "knot_index": knot_index, "cal_block": cal_block, "cal_column": cal_column, "obs_count": obs_count, "src_res": src_res, "att_res": att_res, "cal_res": cal_res, "src_dir": src_dir, "att_dir": att_dir, "cal_dir": cal_dir}


def spline(phase):
    rest = 1.0 - phase
    cube = phase * phase * phase
    square = phase * phase
    first = rest * rest * rest / 6.0
    second = (3.0 * cube - 6.0 * square + 4.0) / 6.0
    third = (-3.0 * cube + 3.0 * square + 3.0 * phase + 1.0) / 6.0
    fourth = cube / 6.0
    return (first, second, third, fourth)


def reference(src_design, att_design, obs_phase, cal_design, obs_weight, knot_index, cal_block, cal_column, obs_count, src_res, att_res, cal_res, src_dir, att_dir, cal_dir):
    live_mask = (jnp.arange(NOBS, dtype=jnp.int32)[None, :] < obs_count[:, None]).astype(jnp.float32)
    basis = spline(obs_phase)
    y_src = jnp.sum(src_design * src_dir[:, :, None], axis=0)
    y_att = jnp.zeros_like(obs_phase)
    for offset in range(4):
        picked = att_dir[:, knot_index + offset]
        y_att = y_att + basis[offset] * jnp.sum(att_design * picked, axis=0)
    flat_index = (cal_block * CW + cal_column).astype(jnp.int32)
    y_cal = cal_design * cal_dir.reshape(-1)[flat_index]
    response = live_mask * (y_src + y_att + y_cal)
    weighted = obs_weight * response
    curvature = jnp.sum(weighted * response)
    q_src = jnp.sum(src_design * weighted[None], axis=2)
    ids = jnp.concatenate([(knot_index + offset).reshape(-1) for offset in range(4)]).astype(jnp.int32)
    data = jnp.concatenate([(basis[offset][None] * att_design * weighted[None]).reshape(3, -1) for offset in range(4)], axis=1)
    q_att = jax.vmap(lambda row: jax.ops.segment_sum(row, ids, num_segments=NKNOT))(data)
    q_cal = jax.ops.segment_sum((cal_design * weighted).reshape(-1), flat_index.reshape(-1), num_segments=NCB * CW).reshape(NCB, CW)
    norm_now = jnp.sum(src_res * src_res) + jnp.sum(att_res * att_res) + jnp.sum(cal_res * cal_res)
    step_len = norm_now / curvature
    new_src_res = src_res - step_len * q_src
    new_att_res = att_res - step_len * q_att
    new_cal_res = cal_res - step_len * q_cal
    norm_next = jnp.sum(new_src_res * new_src_res) + jnp.sum(new_att_res * new_att_res) + jnp.sum(new_cal_res * new_cal_res)
    ratio = norm_next / norm_now
    return (new_src_res, new_att_res, new_cal_res, new_src_res + ratio * src_dir, new_att_res + ratio * att_dir, new_cal_res + ratio * cal_dir)
```

```python
import jax
import jax.numpy as jnp
from jax import lax
from jax.sharding import PartitionSpec as P


EXACT = lax.Precision.HIGHEST


def passed_along(block, axis, distance):
    devices = range(lax.axis_size(axis))
    route = [(i - distance, i) for i in devices if i - distance in devices]
    return lax.ppermute(block, axis, route)


def spline(phase):
    rest = 1.0 - phase
    cube = phase * phase * phase
    square = phase * phase
    first = rest * rest * rest / 6.0
    second = (3.0 * cube - 6.0 * square + 4.0) / 6.0
    third = (-3.0 * cube + 3.0 * square + 3.0 * phase + 1.0) / 6.0
    fourth = cube / 6.0
    return (first, second, third, fourth)


def local(
    src_design,
    att_design,
    obs_phase,
    cal_design,
    obs_weight,
    knot_index,
    cal_block,
    cal_column,
    obs_count,
    src_res,
    att_res,
    cal_res,
    src_dir,
    att_dir,
    cal_dir,
):
    knot_count = att_dir.shape[1]
    blocks, col_width = cal_dir.shape
    all_blocks = blocks * lax.axis_size("cal")
    cal_size = all_blocks * col_width
    lane = 128
    rows = cal_size // lane
    src_rows, slots = obs_phase.shape
    first_row = (lax.axis_index("tm") == 0).astype(jnp.float32)

    cal_values = lax.all_gather(cal_dir, "cal", axis=0, tiled=True)
    edge_knots = passed_along(att_dir[:, :3], ("tm", "cal"), -1)
    att_ext = jnp.concatenate([att_dir, edge_knots], axis=1)

    live_mask = (lax.broadcasted_iota(jnp.int32, obs_phase.shape, 1) < obs_count[:, None]).astype(
        jnp.float32
    )
    basis = spline(obs_phase)
    local_knot = knot_index - lax.axis_index(("tm", "cal")) * knot_count

    knot_iota = lax.broadcasted_iota(jnp.int32, (knot_count, 1, 1), 0)
    knot_hot = (local_knot[None] == knot_iota).astype(jnp.float32)

    table = jnp.stack([att_ext[:, m : m + knot_count].T for m in range(4)], axis=1)
    table = table.reshape(knot_count, 12)
    picked = jnp.einsum("jq,jso->qso", table, knot_hot, precision=EXACT).reshape(4, 3, src_rows, slots)
    y_att = jnp.zeros_like(obs_phase)
    for m in range(4):
        y_att = y_att + basis[m] * jnp.sum(att_design * picked[m], axis=0)

    flat_index = cal_block * col_width + cal_column
    high = flat_index // lane
    low = flat_index % lane
    high_hot = (high[None] == lax.broadcasted_iota(jnp.int32, (rows, 1, 1), 0)).astype(jnp.float32)
    low_hot = (low[None] == lax.broadcasted_iota(jnp.int32, (lane, 1, 1), 0)).astype(jnp.float32)
    cal_table = cal_values.reshape(rows, lane)
    row_vals = jnp.einsum("hl,hso->lso", cal_table, high_hot, precision=EXACT)
    y_cal = cal_design * jnp.sum(row_vals * low_hot, axis=0)

    y_src = jnp.sum(src_design * src_dir[:, :, None], axis=0)
    response = live_mask * (y_src + y_att + y_cal)
    weighted = obs_weight * response
    curv_local = jnp.sum(weighted * response)
    norm_local = (
        jnp.sum(src_res * src_res)
        + jnp.sum(att_res * att_res)
        + first_row * jnp.sum(cal_res * cal_res)
    )
    q_src = jnp.sum(src_design * weighted[None], axis=2)

    scaled = att_design * weighted[None]
    spread = jnp.stack([basis[m][None] * scaled for m in range(4)], axis=0).reshape(12, src_rows, slots)
    gathered = jnp.einsum("qso,jso->jq", spread, knot_hot, precision=EXACT).reshape(knot_count, 4, 3)
    grad_ext = jnp.zeros((3, knot_count + 3), jnp.float32)
    for m in range(4):
        grad_ext = grad_ext + jnp.pad(gathered[:, m, :].T, ((0, 0), (m, 3 - m)))
    incoming = passed_along(grad_ext[:, knot_count:], ("tm", "cal"), 1)
    q_att = jnp.concatenate([grad_ext[:, :3] + incoming, grad_ext[:, 3:knot_count]], axis=1)

    cal_weighted = (cal_design * weighted)[None] * low_hot
    cal_term = jnp.einsum("hso,lso->hl", high_hot, cal_weighted, precision=EXACT)
    scalars = jnp.zeros((1, lane), jnp.float32).at[0, 0].set(norm_local).at[0, 1].set(curv_local)
    packed = jnp.concatenate([cal_term, scalars], axis=0)
    summed = lax.psum(packed, ("tm", "cal"))
    norm_now = summed[rows, 0]
    curvature = summed[rows, 1]
    own = lax.axis_index("cal") * (blocks * col_width // lane)
    q_cal = lax.dynamic_slice_in_dim(summed, own, blocks * col_width // lane, 0).reshape(blocks, col_width)

    step_len = norm_now / curvature
    new_src_res = src_res - step_len * q_src
    new_att_res = att_res - step_len * q_att
    new_cal_res = cal_res - step_len * q_cal
    next_local = (
        jnp.sum(new_src_res * new_src_res)
        + jnp.sum(new_att_res * new_att_res)
        + first_row * jnp.sum(new_cal_res * new_cal_res)
    )
    norm_next = lax.psum(jnp.zeros((1, lane), jnp.float32).at[0, 0].set(next_local), ("tm", "cal"))[0, 0]
    ratio = norm_next / norm_now
    return (
        new_src_res,
        new_att_res,
        new_cal_res,
        new_src_res + ratio * src_dir,
        new_att_res + ratio * att_dir,
        new_cal_res + ratio * cal_dir,
    )


def solution(mesh):
    return jax.shard_map(
        local,
        mesh=mesh,
        in_specs=(
            P(None, ("tm", "cal"), None),
            P(None, ("tm", "cal"), None),
            P(("tm", "cal"), None),
            P(("tm", "cal"), None),
            P(("tm", "cal"), None),
            P(("tm", "cal"), None),
            P(("tm", "cal"), None),
            P(("tm", "cal"), None),
            P(("tm", "cal")),
            P(None, ("tm", "cal")),
            P(None, ("tm", "cal")),
            P("cal", None),
            P(None, ("tm", "cal")),
            P(None, ("tm", "cal")),
            P("cal", None),
        ),
        out_specs=(
            P(None, ("tm", "cal")),
            P(None, ("tm", "cal")),
            P("cal", None),
            P(None, ("tm", "cal")),
            P(None, ("tm", "cal")),
            P("cal", None),
        ),
        check_vma=False,
    )
```

```python
import jax
import jax.numpy as jnp
from jax import lax
from jax.sharding import PartitionSpec as P


EXACT = lax.Precision.HIGHEST


def passed_along(block, axis, distance):
    devices = range(lax.axis_size(axis))
    route = [(i - distance, i) for i in devices if i - distance in devices]
    return lax.ppermute(block, axis, route)


def exchanged(block, axis, distance):
    devices = range(lax.axis_size(axis))
    return lax.ppermute(block, axis, [(i, i ^ distance) for i in devices])


def halving_sum(rows, extra, axis):
    count = lax.axis_size(axis)
    me = lax.axis_index(axis)
    distance = count // 2
    while distance >= 1:
        half = rows.shape[0] // 2
        upper = (me // distance) % 2
        keep = lax.dynamic_slice_in_dim(rows, upper * half, half, 0)
        send = lax.dynamic_slice_in_dim(rows, (1 - upper) * half, half, 0)
        got = exchanged(jnp.concatenate([send, extra], axis=0), axis, distance)
        rows = keep + got[:half]
        extra = extra + got[half:]
        distance //= 2
    return rows, extra


def doubling_sum(rows, axis):
    count = lax.axis_size(axis)
    distance = 1
    while distance < count:
        rows = rows + exchanged(rows, axis, distance)
        distance *= 2
    return rows


def spline(phase):
    rest = 1.0 - phase
    cube = phase * phase * phase
    square = phase * phase
    first = rest * rest * rest / 6.0
    second = (3.0 * cube - 6.0 * square + 4.0) / 6.0
    third = (-3.0 * cube + 3.0 * square + 3.0 * phase + 1.0) / 6.0
    fourth = cube / 6.0
    return (first, second, third, fourth)


def local(
    src_design,
    att_design,
    obs_phase,
    cal_design,
    obs_weight,
    knot_index,
    cal_block,
    cal_column,
    obs_count,
    src_res,
    att_res,
    cal_res,
    src_dir,
    att_dir,
    cal_dir,
):
    knot_count = att_dir.shape[1]
    blocks, col_width = cal_dir.shape
    all_blocks = blocks * lax.axis_size("cal")
    cal_size = all_blocks * col_width
    lane = 128
    rows = cal_size // lane
    src_rows, slots = obs_phase.shape
    first_row = (lax.axis_index("tm") == 0).astype(jnp.float32)

    cal_values = lax.all_gather(cal_dir, "cal", axis=0, tiled=True)
    edge_knots = passed_along(att_dir[:, :3], ("tm", "cal"), -1)
    att_ext = jnp.concatenate([att_dir, edge_knots], axis=1)

    live_mask = (lax.broadcasted_iota(jnp.int32, obs_phase.shape, 1) < obs_count[:, None]).astype(
        jnp.float32
    )
    basis = spline(obs_phase)
    local_knot = knot_index - lax.axis_index(("tm", "cal")) * knot_count

    n_obs = src_rows * slots
    flat = lambda a: a.reshape(1, n_obs)

    knot_hot = (flat(local_knot) == lax.broadcasted_iota(jnp.int32, (knot_count, 1), 0)).astype(jnp.float32)

    table = jnp.stack([att_ext[:, m : m + knot_count] for m in range(4)], axis=0).reshape(12, knot_count)
    picked = jnp.dot(table, knot_hot, precision=EXACT).reshape(4, 3, src_rows, slots)
    y_att = jnp.zeros_like(obs_phase)
    for m in range(4):
        y_att = y_att + basis[m] * jnp.sum(att_design * picked[m], axis=0)

    flat_index = flat(cal_block * col_width + cal_column)
    high_hot = (flat_index // lane == lax.broadcasted_iota(jnp.int32, (rows, 1), 0)).astype(jnp.float32)
    low_hot = (flat_index % lane == lax.broadcasted_iota(jnp.int32, (lane, 1), 0)).astype(jnp.float32)
    cal_table = cal_values.reshape(rows, lane)
    row_vals = lax.dot_general(cal_table, high_hot, (((0,), (0,)), ((), ())), precision=EXACT)
    y_cal = cal_design * jnp.sum(row_vals * low_hot, axis=0).reshape(src_rows, slots)

    y_src = jnp.sum(src_design * src_dir[:, :, None], axis=0)
    response = live_mask * (y_src + y_att + y_cal)
    weighted = obs_weight * response
    curv_local = jnp.sum(weighted * response)
    norm_local = (
        jnp.sum(src_res * src_res)
        + jnp.sum(att_res * att_res)
        + first_row * jnp.sum(cal_res * cal_res)
    )
    q_src = jnp.sum(src_design * weighted[None], axis=2)

    scaled = att_design * weighted[None]
    spread = jnp.stack([basis[m][None] * scaled for m in range(4)], axis=0).reshape(12, n_obs)
    gathered = lax.dot_general(spread, knot_hot, (((1,), (1,)), ((), ())), precision=EXACT)
    gathered = gathered.reshape(4, 3, knot_count)
    grad_ext = jnp.zeros((3, knot_count + 3), jnp.float32)
    for m in range(4):
        grad_ext = grad_ext + jnp.pad(gathered[m], ((0, 0), (m, 3 - m)))
    incoming = passed_along(grad_ext[:, knot_count:], ("tm", "cal"), 1)
    q_att = jnp.concatenate([grad_ext[:, :3] + incoming, grad_ext[:, 3:knot_count]], axis=1)

    cal_weighted = flat(cal_design * weighted) * low_hot
    cal_term = lax.dot_general(high_hot, cal_weighted, (((1,), (1,)), ((), ())), precision=EXACT)
    scalars = jnp.zeros((1, lane), jnp.float32).at[0, 0].set(norm_local).at[0, 1].set(curv_local)
    q_cal, scalars = halving_sum(cal_term, scalars, "cal")
    summed = doubling_sum(jnp.concatenate([q_cal, scalars], axis=0), "tm")
    norm_now = summed[-1, 0]
    curvature = summed[-1, 1]
    q_cal = summed[:-1].reshape(blocks, col_width)

    step_len = norm_now / curvature
    new_src_res = src_res - step_len * q_src
    new_att_res = att_res - step_len * q_att
    new_cal_res = cal_res - step_len * q_cal
    next_local = (
        jnp.sum(new_src_res * new_src_res)
        + jnp.sum(new_att_res * new_att_res)
        + first_row * jnp.sum(new_cal_res * new_cal_res)
    )
    norm_next = jnp.zeros((1, lane), jnp.float32).at[0, 0].set(next_local)
    norm_next = doubling_sum(doubling_sum(norm_next, "cal"), "tm")[0, 0]
    ratio = norm_next / norm_now
    return (
        new_src_res,
        new_att_res,
        new_cal_res,
        new_src_res + ratio * src_dir,
        new_att_res + ratio * att_dir,
        new_cal_res + ratio * cal_dir,
    )


def solution(mesh):
    return jax.shard_map(
        local,
        mesh=mesh,
        in_specs=(
            P(None, ("tm", "cal"), None),
            P(None, ("tm", "cal"), None),
            P(("tm", "cal"), None),
            P(("tm", "cal"), None),
            P(("tm", "cal"), None),
            P(("tm", "cal"), None),
            P(("tm", "cal"), None),
            P(("tm", "cal"), None),
            P(("tm", "cal")),
            P(None, ("tm", "cal")),
            P(None, ("tm", "cal")),
            P("cal", None),
            P(None, ("tm", "cal")),
            P(None, ("tm", "cal")),
            P("cal", None),
        ),
        out_specs=(
            P(None, ("tm", "cal")),
            P(None, ("tm", "cal")),
            P("cal", None),
            P(None, ("tm", "cal")),
            P(None, ("tm", "cal")),
            P("cal", None),
        ),
        check_vma=False,
    )
```

```python
import jax
import jax.numpy as jnp
from jax import lax
from jax.sharding import PartitionSpec as P


EXACT = lax.Precision.HIGHEST


def passed_along(block, axis, distance):
    devices = range(lax.axis_size(axis))
    route = [(i - distance, i) for i in devices if i - distance in devices]
    return lax.ppermute(block, axis, route)


def exchanged(block, axis, distance):
    devices = range(lax.axis_size(axis))
    return lax.ppermute(block, axis, [(i, i ^ distance) for i in devices])


def halving_sum(rows, extra, axis):
    count = lax.axis_size(axis)
    me = lax.axis_index(axis)
    distance = count // 2
    while distance >= 1:
        half = rows.shape[0] // 2
        upper = (me // distance) % 2
        keep = lax.dynamic_slice_in_dim(rows, upper * half, half, 0)
        send = lax.dynamic_slice_in_dim(rows, (1 - upper) * half, half, 0)
        got = exchanged(jnp.concatenate([send, extra], axis=0), axis, distance)
        rows = keep + got[:half]
        extra = extra + got[half:]
        distance //= 2
    return rows, extra


def doubling_sum(rows, axis):
    count = lax.axis_size(axis)
    distance = 1
    while distance < count:
        rows = rows + exchanged(rows, axis, distance)
        distance *= 2
    return rows


def from_all(block, axis):
    count = lax.axis_size(axis)
    me = lax.axis_index(axis)
    got = [block] + [
        lax.ppermute(block, axis, [(i, (i + shift) % count) for i in range(count)])
        for shift in range(1, count)
    ]
    stacked = jnp.stack(got[::-1] + got[::-1], axis=0)
    return lax.dynamic_slice_in_dim(stacked, count - 1 - me, count, 0)


def ordered_sum(parts):
    total = parts[0]
    for k in range(1, parts.shape[0]):
        total = total + parts[k]
    return total


def all_sum(block, axis):
    if lax.axis_size(axis) > 8:
        return doubling_sum(block, axis)
    return ordered_sum(from_all(block, axis))


def scatter_sum(rows, extra, axis):
    count = lax.axis_size(axis)
    if count > 8:
        return halving_sum(rows, extra, axis)
    me = lax.axis_index(axis)
    share = rows.shape[0] // count
    got = []
    for shift in range(count):
        target = (me + shift) % count
        part = jnp.concatenate([lax.dynamic_slice_in_dim(rows, target * share, share, 0), extra], axis=0)
        if shift:
            part = lax.ppermute(part, axis, [(i, (i + shift) % count) for i in range(count)])
        got.append(part)
    stacked = jnp.stack(got[::-1] + got[::-1], axis=0)
    total = ordered_sum(lax.dynamic_slice_in_dim(stacked, count - 1 - me, count, 0))
    return total[:share], total[share:]


def spline(phase):
    rest = 1.0 - phase
    cube = phase * phase * phase
    square = phase * phase
    first = rest * rest * rest / 6.0
    second = (3.0 * cube - 6.0 * square + 4.0) / 6.0
    third = (-3.0 * cube + 3.0 * square + 3.0 * phase + 1.0) / 6.0
    fourth = cube / 6.0
    return (first, second, third, fourth)


def local(
    src_design,
    att_design,
    obs_phase,
    cal_design,
    obs_weight,
    knot_index,
    cal_block,
    cal_column,
    obs_count,
    src_res,
    att_res,
    cal_res,
    src_dir,
    att_dir,
    cal_dir,
):
    knot_count = att_dir.shape[1]
    blocks, col_width = cal_dir.shape
    all_blocks = blocks * lax.axis_size("cal")
    cal_size = all_blocks * col_width
    lane = 128
    rows = cal_size // lane
    src_rows, slots = obs_phase.shape
    first_row = (lax.axis_index("tm") == 0).astype(jnp.float32)

    cal_values = from_all(cal_dir, "cal").reshape(all_blocks, col_width)
    edge_knots = passed_along(att_dir[:, :3], ("tm", "cal"), -1)
    att_ext = jnp.concatenate([att_dir, edge_knots], axis=1)

    live_mask = (lax.broadcasted_iota(jnp.int32, obs_phase.shape, 1) < obs_count[:, None]).astype(
        jnp.float32
    )
    basis = spline(obs_phase)
    local_knot = knot_index - lax.axis_index(("tm", "cal")) * knot_count

    n_obs = src_rows * slots
    flat = lambda a: a.reshape(1, n_obs)

    knot_hot = (flat(local_knot) == lax.broadcasted_iota(jnp.int32, (knot_count, 1), 0)).astype(jnp.float32)

    table = jnp.stack([att_ext[:, m : m + knot_count] for m in range(4)], axis=0).reshape(12, knot_count)
    picked = jnp.dot(table, knot_hot, precision=EXACT).reshape(4, 3, src_rows, slots)
    y_att = jnp.zeros_like(obs_phase)
    for m in range(4):
        y_att = y_att + basis[m] * jnp.sum(att_design * picked[m], axis=0)

    flat_index = flat(cal_block * col_width + cal_column)
    high_hot = (flat_index // lane == lax.broadcasted_iota(jnp.int32, (rows, 1), 0)).astype(jnp.float32)
    low_hot = (flat_index % lane == lax.broadcasted_iota(jnp.int32, (lane, 1), 0)).astype(jnp.float32)
    cal_table = cal_values.reshape(rows, lane)
    row_vals = lax.dot_general(cal_table, high_hot, (((0,), (0,)), ((), ())), precision=EXACT)
    y_cal = cal_design * jnp.sum(row_vals * low_hot, axis=0).reshape(src_rows, slots)

    y_src = jnp.sum(src_design * src_dir[:, :, None], axis=0)
    response = live_mask * (y_src + y_att + y_cal)
    weighted = obs_weight * response
    curv_local = jnp.sum(weighted * response)
    norm_local = (
        jnp.sum(src_res * src_res)
        + jnp.sum(att_res * att_res)
        + first_row * jnp.sum(cal_res * cal_res)
    )
    q_src = jnp.sum(src_design * weighted[None], axis=2)

    scaled = att_design * weighted[None]
    spread = jnp.stack([basis[m][None] * scaled for m in range(4)], axis=0).reshape(12, n_obs)
    gathered = lax.dot_general(spread, knot_hot, (((1,), (1,)), ((), ())), precision=EXACT)
    gathered = gathered.reshape(4, 3, knot_count)
    grad_ext = jnp.zeros((3, knot_count + 3), jnp.float32)
    for m in range(4):
        grad_ext = grad_ext + jnp.pad(gathered[m], ((0, 0), (m, 3 - m)))
    incoming = passed_along(grad_ext[:, knot_count:], ("tm", "cal"), 1)
    q_att = jnp.concatenate([grad_ext[:, :3] + incoming, grad_ext[:, 3:knot_count]], axis=1)

    cal_weighted = flat(cal_design * weighted) * low_hot
    cal_term = lax.dot_general(high_hot, cal_weighted, (((1,), (1,)), ((), ())), precision=EXACT)
    scalars = jnp.zeros((1, lane), jnp.float32).at[0, 0].set(norm_local).at[0, 1].set(curv_local)
    q_cal, scalars = scatter_sum(cal_term, scalars, "cal")
    summed = all_sum(jnp.concatenate([q_cal, scalars], axis=0), "tm")
    norm_now = summed[-1, 0]
    curvature = summed[-1, 1]
    q_cal = summed[:-1].reshape(blocks, col_width)

    step_len = norm_now / curvature
    new_src_res = src_res - step_len * q_src
    new_att_res = att_res - step_len * q_att
    new_cal_res = cal_res - step_len * q_cal
    next_local = (
        jnp.sum(new_src_res * new_src_res)
        + jnp.sum(new_att_res * new_att_res)
        + first_row * jnp.sum(new_cal_res * new_cal_res)
    )
    norm_next = jnp.zeros((1, lane), jnp.float32).at[0, 0].set(next_local)
    norm_next = all_sum(all_sum(norm_next, "cal"), "tm")[0, 0]
    ratio = norm_next / norm_now
    return (
        new_src_res,
        new_att_res,
        new_cal_res,
        new_src_res + ratio * src_dir,
        new_att_res + ratio * att_dir,
        new_cal_res + ratio * cal_dir,
    )


def solution(mesh):
    return jax.shard_map(
        local,
        mesh=mesh,
        in_specs=(
            P(None, ("tm", "cal"), None),
            P(None, ("tm", "cal"), None),
            P(("tm", "cal"), None),
            P(("tm", "cal"), None),
            P(("tm", "cal"), None),
            P(("tm", "cal"), None),
            P(("tm", "cal"), None),
            P(("tm", "cal"), None),
            P(("tm", "cal")),
            P(None, ("tm", "cal")),
            P(None, ("tm", "cal")),
            P("cal", None),
            P(None, ("tm", "cal")),
            P(None, ("tm", "cal")),
            P("cal", None),
        ),
        out_specs=(
            P(None, ("tm", "cal")),
            P(None, ("tm", "cal")),
            P("cal", None),
            P(None, ("tm", "cal")),
            P(None, ("tm", "cal")),
            P("cal", None),
        ),
        check_vma=False,
    )
```

```python
import jax
import jax.numpy as jnp
from jax import lax
from jax.sharding import PartitionSpec as P


EXACT = lax.Precision.HIGHEST


def passed_along(block, axis, distance):
    devices = range(lax.axis_size(axis))
    route = [(i - distance, i) for i in devices if i - distance in devices]
    return lax.ppermute(block, axis, route)


def exchanged(block, axis, distance):
    devices = range(lax.axis_size(axis))
    return lax.ppermute(block, axis, [(i, i ^ distance) for i in devices])


def halving_sum(rows, extra, axis):
    count = lax.axis_size(axis)
    me = lax.axis_index(axis)
    distance = count // 2
    while distance >= 1:
        half = rows.shape[0] // 2
        upper = (me // distance) % 2
        keep = lax.dynamic_slice_in_dim(rows, upper * half, half, 0)
        send = lax.dynamic_slice_in_dim(rows, (1 - upper) * half, half, 0)
        got = exchanged(jnp.concatenate([send, extra], axis=0), axis, distance)
        rows = keep + got[:half]
        extra = extra + got[half:]
        distance //= 2
    return rows, extra


def doubling_sum(rows, axis):
    count = lax.axis_size(axis)
    distance = 1
    while distance < count:
        rows = rows + exchanged(rows, axis, distance)
        distance *= 2
    return rows


def spline(phase):
    rest = 1.0 - phase
    cube = phase * phase * phase
    square = phase * phase
    first = rest * rest * rest / 6.0
    second = (3.0 * cube - 6.0 * square + 4.0) / 6.0
    third = (-3.0 * cube + 3.0 * square + 3.0 * phase + 1.0) / 6.0
    fourth = cube / 6.0
    return (first, second, third, fourth)


def local(
    src_design,
    att_design,
    obs_phase,
    cal_design,
    obs_weight,
    knot_index,
    cal_block,
    cal_column,
    obs_count,
    src_res,
    att_res,
    cal_res,
    src_dir,
    att_dir,
    cal_dir,
):
    knot_count = att_dir.shape[1]
    blocks, col_width = cal_dir.shape
    all_blocks = blocks * lax.axis_size("cal")
    cal_size = all_blocks * col_width
    lane = 128
    rows = cal_size // lane
    src_rows, slots = obs_phase.shape

    cal_both = lax.all_gather(jnp.stack([cal_dir, cal_res]), "cal", axis=1, tiled=True)
    cal_values = cal_both[0]
    cal_res_all = cal_both[1]
    edge_knots = passed_along(att_dir[:, :3], ("tm", "cal"), -1)
    att_ext = jnp.concatenate([att_dir, edge_knots], axis=1)

    live_mask = (lax.broadcasted_iota(jnp.int32, obs_phase.shape, 1) < obs_count[:, None]).astype(
        jnp.float32
    )
    basis = spline(obs_phase)
    local_knot = knot_index - lax.axis_index(("tm", "cal")) * knot_count

    n_obs = src_rows * slots
    flat = lambda a: a.reshape(1, n_obs)

    knot_hot = (flat(local_knot) == lax.broadcasted_iota(jnp.int32, (knot_count, 1), 0)).astype(jnp.float32)

    table = jnp.stack([att_ext[:, m : m + knot_count] for m in range(4)], axis=0).reshape(12, knot_count)
    picked = jnp.dot(table, knot_hot, precision=EXACT).reshape(4, 3, src_rows, slots)
    y_att = jnp.zeros_like(obs_phase)
    for m in range(4):
        y_att = y_att + basis[m] * jnp.sum(att_design * picked[m], axis=0)

    flat_index = flat(cal_block * col_width + cal_column)
    high_hot = (flat_index // lane == lax.broadcasted_iota(jnp.int32, (rows, 1), 0)).astype(jnp.float32)
    low_hot = (flat_index % lane == lax.broadcasted_iota(jnp.int32, (lane, 1), 0)).astype(jnp.float32)
    cal_table = cal_values.reshape(rows, lane)
    row_vals = lax.dot_general(cal_table, high_hot, (((0,), (0,)), ((), ())), precision=EXACT)
    y_cal = cal_design * jnp.sum(row_vals * low_hot, axis=0).reshape(src_rows, slots)

    y_src = jnp.sum(src_design * src_dir[:, :, None], axis=0)
    response = live_mask * (y_src + y_att + y_cal)
    weighted = obs_weight * response
    curv_local = jnp.sum(weighted * response)
    q_src = jnp.sum(src_design * weighted[None], axis=2)

    scaled = att_design * weighted[None]
    spread = jnp.stack([basis[m][None] * scaled for m in range(4)], axis=0).reshape(12, n_obs)
    gathered = lax.dot_general(spread, knot_hot, (((1,), (1,)), ((), ())), precision=EXACT)
    gathered = gathered.reshape(4, 3, knot_count)
    grad_ext = jnp.zeros((3, knot_count + 3), jnp.float32)
    for m in range(4):
        grad_ext = grad_ext + jnp.pad(gathered[m], ((0, 0), (m, 3 - m)))
    incoming = passed_along(grad_ext[:, knot_count:], ("tm", "cal"), 1)
    q_att = jnp.concatenate([grad_ext[:, :3] + incoming, grad_ext[:, 3:knot_count]], axis=1)

    cal_weighted = flat(cal_design * weighted) * low_hot
    cal_term = lax.dot_general(high_hot, cal_weighted, (((1,), (1,)), ((), ())), precision=EXACT)
    res_sq = jnp.sum(src_res * src_res) + jnp.sum(att_res * att_res)
    res_q = jnp.sum(src_res * q_src) + jnp.sum(att_res * q_att)
    q_sq = jnp.sum(q_src * q_src) + jnp.sum(q_att * q_att)
    scalars = jnp.zeros((1, lane), jnp.float32)
    scalars = scalars.at[0, 0].set(res_sq).at[0, 1].set(curv_local)
    scalars = scalars.at[0, 2].set(res_q).at[0, 3].set(q_sq)
    summed = doubling_sum(doubling_sum(jnp.concatenate([cal_term, scalars], axis=0), "cal"), "tm")
    res_sq, curvature, res_q, q_sq = (summed[rows, k] for k in range(4))
    q_cal_all = summed[:rows].reshape(all_blocks, col_width)

    norm_now = res_sq + jnp.sum(cal_res_all * cal_res_all)
    step_len = norm_now / curvature
    new_src_res = src_res - step_len * q_src
    new_att_res = att_res - step_len * q_att
    new_cal_all = cal_res_all - step_len * q_cal_all
    kept = res_sq - step_len * (2.0 * res_q - step_len * q_sq)
    norm_next = kept + jnp.sum(new_cal_all * new_cal_all)
    ratio = norm_next / norm_now
    new_cal_res = lax.dynamic_slice_in_dim(new_cal_all, lax.axis_index("cal") * blocks, blocks, 0)
    return (
        new_src_res,
        new_att_res,
        new_cal_res,
        new_src_res + ratio * src_dir,
        new_att_res + ratio * att_dir,
        new_cal_res + ratio * cal_dir,
    )


def solution(mesh):
    return jax.shard_map(
        local,
        mesh=mesh,
        in_specs=(
            P(None, ("tm", "cal"), None),
            P(None, ("tm", "cal"), None),
            P(("tm", "cal"), None),
            P(("tm", "cal"), None),
            P(("tm", "cal"), None),
            P(("tm", "cal"), None),
            P(("tm", "cal"), None),
            P(("tm", "cal"), None),
            P(("tm", "cal")),
            P(None, ("tm", "cal")),
            P(None, ("tm", "cal")),
            P("cal", None),
            P(None, ("tm", "cal")),
            P(None, ("tm", "cal")),
            P("cal", None),
        ),
        out_specs=(
            P(None, ("tm", "cal")),
            P(None, ("tm", "cal")),
            P("cal", None),
            P(None, ("tm", "cal")),
            P(None, ("tm", "cal")),
            P("cal", None),
        ),
        check_vma=False,
    )
```

```python
import jax
import jax.numpy as jnp
from jax import lax
from jax.sharding import PartitionSpec as P


EXACT = lax.Precision.HIGHEST


def passed_along(block, axis, distance):
    devices = range(lax.axis_size(axis))
    route = [(i - distance, i) for i in devices if i - distance in devices]
    return lax.ppermute(block, axis, route)


def exchanged(block, axis, distance):
    devices = range(lax.axis_size(axis))
    return lax.ppermute(block, axis, [(i, i ^ distance) for i in devices])


def halving_sum(rows, extra, axis):
    count = lax.axis_size(axis)
    me = lax.axis_index(axis)
    distance = count // 2
    while distance >= 1:
        half = rows.shape[0] // 2
        upper = (me // distance) % 2
        keep = lax.dynamic_slice_in_dim(rows, upper * half, half, 0)
        send = lax.dynamic_slice_in_dim(rows, (1 - upper) * half, half, 0)
        got = exchanged(jnp.concatenate([send, extra], axis=0), axis, distance)
        rows = keep + got[:half]
        extra = extra + got[half:]
        distance //= 2
    return rows, extra


def doubling_sum(rows, axis):
    count = lax.axis_size(axis)
    distance = 1
    while distance < count:
        rows = rows + exchanged(rows, axis, distance)
        distance *= 2
    return rows


def spline(phase):
    rest = 1.0 - phase
    cube = phase * phase * phase
    square = phase * phase
    first = rest * rest * rest / 6.0
    second = (3.0 * cube - 6.0 * square + 4.0) / 6.0
    third = (-3.0 * cube + 3.0 * square + 3.0 * phase + 1.0) / 6.0
    fourth = cube / 6.0
    return (first, second, third, fourth)


def local(
    src_design,
    att_design,
    obs_phase,
    cal_design,
    obs_weight,
    knot_index,
    cal_block,
    cal_column,
    obs_count,
    src_res,
    att_res,
    cal_res,
    src_dir,
    att_dir,
    cal_dir,
):
    knot_count = att_dir.shape[1]
    blocks, col_width = cal_dir.shape
    all_blocks = blocks * lax.axis_size("cal")
    cal_size = all_blocks * col_width
    lane = 128
    rows = cal_size // lane
    src_rows, slots = obs_phase.shape

    cal_both = lax.all_gather(jnp.stack([cal_dir, cal_res]), "cal", axis=1, tiled=True)
    cal_values = cal_both[0]
    cal_res_all = cal_both[1]
    edge_knots = passed_along(att_dir[:, :3], ("tm", "cal"), -1)
    att_ext = jnp.concatenate([att_dir, edge_knots], axis=1)

    live_mask = (lax.broadcasted_iota(jnp.int32, obs_phase.shape, 1) < obs_count[:, None]).astype(
        jnp.float32
    )
    basis = spline(obs_phase)
    local_knot = knot_index - lax.axis_index(("tm", "cal")) * knot_count

    n_obs = src_rows * slots
    flat = lambda a: a.reshape(1, n_obs)

    knot_hot = (flat(local_knot) == lax.broadcasted_iota(jnp.int32, (knot_count, 1), 0)).astype(jnp.float32)

    table = jnp.stack([att_ext[:, m : m + knot_count] for m in range(4)], axis=0).reshape(12, knot_count)
    picked = jnp.dot(table, knot_hot, precision=EXACT).reshape(4, 3, src_rows, slots)
    y_att = jnp.zeros_like(obs_phase)
    for m in range(4):
        y_att = y_att + basis[m] * jnp.sum(att_design * picked[m], axis=0)

    flat_index = flat(cal_block * col_width + cal_column)
    high_hot = (flat_index // lane == lax.broadcasted_iota(jnp.int32, (rows, 1), 0)).astype(jnp.float32)
    low_hot = (flat_index % lane == lax.broadcasted_iota(jnp.int32, (lane, 1), 0)).astype(jnp.float32)
    cal_table = cal_values.reshape(rows, lane)
    row_vals = lax.dot_general(cal_table, high_hot, (((0,), (0,)), ((), ())), precision=EXACT)
    y_cal = cal_design * jnp.sum(row_vals * low_hot, axis=0).reshape(src_rows, slots)

    y_src = jnp.sum(src_design * src_dir[:, :, None], axis=0)
    response = live_mask * (y_src + y_att + y_cal)
    weighted = obs_weight * response
    curv_local = jnp.sum(weighted * response)
    q_src = jnp.sum(src_design * weighted[None], axis=2)

    scaled = att_design * weighted[None]
    spread = jnp.stack([basis[m][None] * scaled for m in range(4)], axis=0).reshape(12, n_obs)
    gathered = lax.dot_general(spread, knot_hot, (((1,), (1,)), ((), ())), precision=EXACT)
    gathered = gathered.reshape(4, 3, knot_count)
    grad_ext = jnp.zeros((3, knot_count + 3), jnp.float32)
    for m in range(4):
        grad_ext = grad_ext + jnp.pad(gathered[m], ((0, 0), (m, 3 - m)))
    incoming = passed_along(grad_ext[:, knot_count:], ("tm", "cal"), 1)
    q_att = jnp.concatenate([grad_ext[:, :3] + incoming, grad_ext[:, 3:knot_count]], axis=1)

    cal_weighted = flat(cal_design * weighted) * low_hot
    cal_term = lax.dot_general(high_hot, cal_weighted, (((1,), (1,)), ((), ())), precision=EXACT)
    res_sq = jnp.sum(src_res * src_res) + jnp.sum(att_res * att_res)
    res_q = jnp.sum(src_res * q_src) + jnp.sum(att_res * q_att)
    q_sq = jnp.sum(q_src * q_src) + jnp.sum(q_att * q_att)
    scalars = jnp.stack([res_sq, curv_local, res_q, q_sq])
    scalars = jnp.concatenate([scalars, jnp.zeros((lane - 4,), jnp.float32)]).reshape(1, lane)
    summed = doubling_sum(doubling_sum(jnp.concatenate([cal_term, scalars], axis=0), "cal"), "tm")
    res_sq, curvature, res_q, q_sq = (summed[rows, k] for k in range(4))
    q_cal_all = summed[:rows].reshape(all_blocks, col_width)

    norm_now = res_sq + jnp.sum(cal_res_all * cal_res_all)
    step_len = norm_now / curvature
    new_src_res = src_res - step_len * q_src
    new_att_res = att_res - step_len * q_att
    new_cal_all = cal_res_all - step_len * q_cal_all
    kept = res_sq - step_len * (2.0 * res_q - step_len * q_sq)
    norm_next = kept + jnp.sum(new_cal_all * new_cal_all)
    ratio = norm_next / norm_now
    new_cal_res = lax.dynamic_slice_in_dim(new_cal_all, lax.axis_index("cal") * blocks, blocks, 0)
    return (
        new_src_res,
        new_att_res,
        new_cal_res,
        new_src_res + ratio * src_dir,
        new_att_res + ratio * att_dir,
        new_cal_res + ratio * cal_dir,
    )


def solution(mesh):
    return jax.shard_map(
        local,
        mesh=mesh,
        in_specs=(
            P(None, ("tm", "cal"), None),
            P(None, ("tm", "cal"), None),
            P(("tm", "cal"), None),
            P(("tm", "cal"), None),
            P(("tm", "cal"), None),
            P(("tm", "cal"), None),
            P(("tm", "cal"), None),
            P(("tm", "cal"), None),
            P(("tm", "cal")),
            P(None, ("tm", "cal")),
            P(None, ("tm", "cal")),
            P("cal", None),
            P(None, ("tm", "cal")),
            P(None, ("tm", "cal")),
            P("cal", None),
        ),
        out_specs=(
            P(None, ("tm", "cal")),
            P(None, ("tm", "cal")),
            P("cal", None),
            P(None, ("tm", "cal")),
            P(None, ("tm", "cal")),
            P("cal", None),
        ),
        check_vma=False,
    )
```

```python
import jax
import jax.numpy as jnp
from jax import lax
from jax.sharding import PartitionSpec as P


EXACT = lax.Precision.HIGHEST


def passed_along(block, axis, distance):
    devices = range(lax.axis_size(axis))
    route = [(i - distance, i) for i in devices if i - distance in devices]
    return lax.ppermute(block, axis, route)


def exchanged(block, axis, distance):
    devices = range(lax.axis_size(axis))
    return lax.ppermute(block, axis, [(i, i ^ distance) for i in devices])


def halving_sum(rows, extra, axis):
    count = lax.axis_size(axis)
    me = lax.axis_index(axis)
    distance = count // 2
    while distance >= 1:
        half = rows.shape[0] // 2
        upper = (me // distance) % 2
        keep = lax.dynamic_slice_in_dim(rows, upper * half, half, 0)
        send = lax.dynamic_slice_in_dim(rows, (1 - upper) * half, half, 0)
        got = exchanged(jnp.concatenate([send, extra], axis=0), axis, distance)
        rows = keep + got[:half]
        extra = extra + got[half:]
        distance //= 2
    return rows, extra


def doubling_sum(rows, axis):
    count = lax.axis_size(axis)
    distance = 1
    while distance < count:
        rows = rows + exchanged(rows, axis, distance)
        distance *= 2
    return rows


def doubling_gather(block, axis):
    count = lax.axis_size(axis)
    me = lax.axis_index(axis)
    distance = 1
    while distance < count:
        other = exchanged(block, axis, distance)
        mine_first = (me // distance) % 2 == 0
        block = jnp.where(
            mine_first,
            jnp.concatenate([block, other], axis=1),
            jnp.concatenate([other, block], axis=1),
        )
        distance *= 2
    return block


def spline(phase):
    rest = 1.0 - phase
    cube = phase * phase * phase
    square = phase * phase
    first = rest * rest * rest / 6.0
    second = (3.0 * cube - 6.0 * square + 4.0) / 6.0
    third = (-3.0 * cube + 3.0 * square + 3.0 * phase + 1.0) / 6.0
    fourth = cube / 6.0
    return (first, second, third, fourth)


def local(
    src_design,
    att_design,
    obs_phase,
    cal_design,
    obs_weight,
    knot_index,
    cal_block,
    cal_column,
    obs_count,
    src_res,
    att_res,
    cal_res,
    src_dir,
    att_dir,
    cal_dir,
):
    knot_count = att_dir.shape[1]
    blocks, col_width = cal_dir.shape
    all_blocks = blocks * lax.axis_size("cal")
    cal_size = all_blocks * col_width
    lane = 128
    rows = cal_size // lane
    src_rows, slots = obs_phase.shape

    cal_both = doubling_gather(jnp.stack([cal_dir, cal_res]), "cal")
    cal_values = cal_both[0]
    cal_res_all = cal_both[1]
    edge_knots = passed_along(att_dir[:, :3], ("tm", "cal"), -1)
    att_ext = jnp.concatenate([att_dir, edge_knots], axis=1)

    live_mask = (lax.broadcasted_iota(jnp.int32, obs_phase.shape, 1) < obs_count[:, None]).astype(
        jnp.float32
    )
    basis = spline(obs_phase)
    local_knot = knot_index - lax.axis_index(("tm", "cal")) * knot_count

    n_obs = src_rows * slots
    flat = lambda a: a.reshape(1, n_obs)

    knot_hot = (flat(local_knot) == lax.broadcasted_iota(jnp.int32, (knot_count, 1), 0)).astype(jnp.float32)

    table = jnp.stack([att_ext[:, m : m + knot_count] for m in range(4)], axis=0).reshape(12, knot_count)
    picked = jnp.dot(table, knot_hot, precision=EXACT).reshape(4, 3, src_rows, slots)
    y_att = jnp.zeros_like(obs_phase)
    for m in range(4):
        y_att = y_att + basis[m] * jnp.sum(att_design * picked[m], axis=0)

    flat_index = flat(cal_block * col_width + cal_column)
    high_hot = (flat_index // lane == lax.broadcasted_iota(jnp.int32, (rows, 1), 0)).astype(jnp.float32)
    low_hot = (flat_index % lane == lax.broadcasted_iota(jnp.int32, (lane, 1), 0)).astype(jnp.float32)
    cal_table = cal_values.reshape(rows, lane)
    row_vals = lax.dot_general(cal_table, high_hot, (((0,), (0,)), ((), ())), precision=EXACT)
    y_cal = cal_design * jnp.sum(row_vals * low_hot, axis=0).reshape(src_rows, slots)

    y_src = jnp.sum(src_design * src_dir[:, :, None], axis=0)
    response = live_mask * (y_src + y_att + y_cal)
    weighted = obs_weight * response
    curv_local = jnp.sum(weighted * response)
    q_src = jnp.sum(src_design * weighted[None], axis=2)

    scaled = att_design * weighted[None]
    spread = jnp.stack([basis[m][None] * scaled for m in range(4)], axis=0).reshape(12, n_obs)
    gathered = lax.dot_general(spread, knot_hot, (((1,), (1,)), ((), ())), precision=EXACT)
    gathered = gathered.reshape(4, 3, knot_count)
    grad_ext = jnp.zeros((3, knot_count + 3), jnp.float32)
    for m in range(4):
        grad_ext = grad_ext + jnp.pad(gathered[m], ((0, 0), (m, 3 - m)))
    incoming = passed_along(grad_ext[:, knot_count:], ("tm", "cal"), 1)
    q_att = jnp.concatenate([grad_ext[:, :3] + incoming, grad_ext[:, 3:knot_count]], axis=1)

    cal_weighted = flat(cal_design * weighted) * low_hot
    cal_term = lax.dot_general(high_hot, cal_weighted, (((1,), (1,)), ((), ())), precision=EXACT)
    res_sq = jnp.sum(src_res * src_res) + jnp.sum(att_res * att_res)
    res_q = jnp.sum(src_res * q_src) + jnp.sum(att_res * q_att)
    q_sq = jnp.sum(q_src * q_src) + jnp.sum(q_att * q_att)
    scalars = jnp.stack([res_sq, curv_local, res_q, q_sq])
    scalars = jnp.concatenate([scalars, jnp.zeros((lane - 4,), jnp.float32)]).reshape(1, lane)
    summed = doubling_sum(doubling_sum(jnp.concatenate([cal_term, scalars], axis=0), "cal"), "tm")
    res_sq, curvature, res_q, q_sq = (summed[rows, k] for k in range(4))
    q_cal_all = summed[:rows].reshape(all_blocks, col_width)

    norm_now = res_sq + jnp.sum(cal_res_all * cal_res_all)
    step_len = norm_now / curvature
    new_src_res = src_res - step_len * q_src
    new_att_res = att_res - step_len * q_att
    new_cal_all = cal_res_all - step_len * q_cal_all
    kept = res_sq - step_len * (2.0 * res_q - step_len * q_sq)
    norm_next = kept + jnp.sum(new_cal_all * new_cal_all)
    ratio = norm_next / norm_now
    new_cal_res = lax.dynamic_slice_in_dim(new_cal_all, lax.axis_index("cal") * blocks, blocks, 0)
    return (
        new_src_res,
        new_att_res,
        new_cal_res,
        new_src_res + ratio * src_dir,
        new_att_res + ratio * att_dir,
        new_cal_res + ratio * cal_dir,
    )


def solution(mesh):
    return jax.shard_map(
        local,
        mesh=mesh,
        in_specs=(
            P(None, ("tm", "cal"), None),
            P(None, ("tm", "cal"), None),
            P(("tm", "cal"), None),
            P(("tm", "cal"), None),
            P(("tm", "cal"), None),
            P(("tm", "cal"), None),
            P(("tm", "cal"), None),
            P(("tm", "cal"), None),
            P(("tm", "cal")),
            P(None, ("tm", "cal")),
            P(None, ("tm", "cal")),
            P("cal", None),
            P(None, ("tm", "cal")),
            P(None, ("tm", "cal")),
            P("cal", None),
        ),
        out_specs=(
            P(None, ("tm", "cal")),
            P(None, ("tm", "cal")),
            P("cal", None),
            P(None, ("tm", "cal")),
            P(None, ("tm", "cal")),
            P("cal", None),
        ),
        check_vma=False,
    )
```

```python
import jax
import jax.numpy as jnp
from jax import lax
from jax.sharding import PartitionSpec as P


EXACT = lax.Precision.HIGHEST


def passed_along(block, axis, distance):
    devices = range(lax.axis_size(axis))
    route = [(i - distance, i) for i in devices if i - distance in devices]
    return lax.ppermute(block, axis, route)


def exchanged(block, axis, distance):
    devices = range(lax.axis_size(axis))
    return lax.ppermute(block, axis, [(i, i ^ distance) for i in devices])


def halving_sum(rows, extra, axis):
    count = lax.axis_size(axis)
    me = lax.axis_index(axis)
    distance = count // 2
    while distance >= 1:
        half = rows.shape[0] // 2
        upper = (me // distance) % 2
        keep = lax.dynamic_slice_in_dim(rows, upper * half, half, 0)
        send = lax.dynamic_slice_in_dim(rows, (1 - upper) * half, half, 0)
        got = exchanged(jnp.concatenate([send, extra], axis=0), axis, distance)
        rows = keep + got[:half]
        extra = extra + got[half:]
        distance //= 2
    return rows, extra


def doubling_sum(rows, axis):
    count = lax.axis_size(axis)
    distance = 1
    while distance < count:
        rows = rows + exchanged(rows, axis, distance)
        distance *= 2
    return rows


def doubling_gather(block, axis):
    count = lax.axis_size(axis)
    me = lax.axis_index(axis)
    distance = 1
    while distance < count:
        other = exchanged(block, axis, distance)
        mine_first = (me // distance) % 2 == 0
        block = jnp.where(
            mine_first,
            jnp.concatenate([block, other], axis=1),
            jnp.concatenate([other, block], axis=1),
        )
        distance *= 2
    return block


def in_thirds(values):
    parts = []
    rest = values
    for _ in range(3):
        head = lax.reduce_precision(rest, exponent_bits=8, mantissa_bits=7)
        parts.append(head.astype(jnp.bfloat16))
        rest = rest - head
    return parts


def spline(phase):
    rest = 1.0 - phase
    cube = phase * phase * phase
    square = phase * phase
    first = rest * rest * rest / 6.0
    second = (3.0 * cube - 6.0 * square + 4.0) / 6.0
    third = (-3.0 * cube + 3.0 * square + 3.0 * phase + 1.0) / 6.0
    fourth = cube / 6.0
    return (first, second, third, fourth)


def local(
    src_design,
    att_design,
    obs_phase,
    cal_design,
    obs_weight,
    knot_index,
    cal_block,
    cal_column,
    obs_count,
    src_res,
    att_res,
    cal_res,
    src_dir,
    att_dir,
    cal_dir,
):
    knot_count = att_dir.shape[1]
    blocks, col_width = cal_dir.shape
    all_blocks = blocks * lax.axis_size("cal")
    cal_size = all_blocks * col_width
    lane = 128
    rows = cal_size // lane
    src_rows, slots = obs_phase.shape

    cal_both = doubling_gather(jnp.stack([cal_dir, cal_res]), "cal")
    cal_values = cal_both[0]
    cal_res_all = cal_both[1]
    edge_knots = passed_along(att_dir[:, :3], ("tm", "cal"), -1)
    att_ext = jnp.concatenate([att_dir, edge_knots], axis=1)

    live_mask = (lax.broadcasted_iota(jnp.int32, obs_phase.shape, 1) < obs_count[:, None]).astype(
        jnp.float32
    )
    basis = spline(obs_phase)
    local_knot = knot_index - lax.axis_index(("tm", "cal")) * knot_count

    n_obs = src_rows * slots
    flat = lambda a: a.reshape(1, n_obs)

    knot_hot = (flat(local_knot) == lax.broadcasted_iota(jnp.int32, (knot_count, 1), 0)).astype(jnp.float32)

    table = jnp.stack([att_ext[:, m : m + knot_count] for m in range(4)], axis=0).reshape(12, knot_count)
    picked = jnp.dot(table, knot_hot, precision=EXACT).reshape(4, 3, src_rows, slots)
    y_att = jnp.zeros_like(obs_phase)
    for m in range(4):
        y_att = y_att + basis[m] * jnp.sum(att_design * picked[m], axis=0)

    flat_index = flat(cal_block * col_width + cal_column)
    high_hot = (flat_index // lane == lax.broadcasted_iota(jnp.int32, (rows, 1), 0)).astype(jnp.bfloat16)
    low_hot = (flat_index % lane == lax.broadcasted_iota(jnp.int32, (lane, 1), 0)).astype(jnp.bfloat16)
    cal_table = cal_values.reshape(rows, lane)
    table_parts = jnp.concatenate([part.T for part in in_thirds(cal_table)], axis=0)
    row_vals = jnp.dot(table_parts, high_hot, preferred_element_type=jnp.float32)
    row_vals = row_vals.reshape(3, lane, n_obs) * low_hot.astype(jnp.float32)[None]
    y_cal = cal_design * jnp.sum(row_vals, axis=(0, 1)).reshape(src_rows, slots)

    y_src = jnp.sum(src_design * src_dir[:, :, None], axis=0)
    response = live_mask * (y_src + y_att + y_cal)
    weighted = obs_weight * response
    curv_local = jnp.sum(weighted * response)
    q_src = jnp.sum(src_design * weighted[None], axis=2)

    scaled = att_design * weighted[None]
    spread = jnp.stack([basis[m][None] * scaled for m in range(4)], axis=0).reshape(12, n_obs)
    gathered = lax.dot_general(spread, knot_hot, (((1,), (1,)), ((), ())), precision=EXACT)
    gathered = gathered.reshape(4, 3, knot_count)
    grad_ext = jnp.zeros((3, knot_count + 3), jnp.float32)
    for m in range(4):
        grad_ext = grad_ext + jnp.pad(gathered[m], ((0, 0), (m, 3 - m)))
    incoming = passed_along(grad_ext[:, knot_count:], ("tm", "cal"), 1)
    q_att = jnp.concatenate([grad_ext[:, :3] + incoming, grad_ext[:, 3:knot_count]], axis=1)

    cal_weighted = jnp.concatenate([low_hot * part for part in in_thirds(flat(cal_design * weighted))], axis=0)
    cal_term = lax.dot_general(
        high_hot, cal_weighted, (((1,), (1,)), ((), ())), preferred_element_type=jnp.float32
    )
    cal_term = cal_term[:, :lane] + cal_term[:, lane : 2 * lane] + cal_term[:, 2 * lane :]
    res_sq = jnp.sum(src_res * src_res) + jnp.sum(att_res * att_res)
    res_q = jnp.sum(src_res * q_src) + jnp.sum(att_res * q_att)
    q_sq = jnp.sum(q_src * q_src) + jnp.sum(q_att * q_att)
    scalars = jnp.stack([res_sq, curv_local, res_q, q_sq])
    scalars = jnp.concatenate([scalars, jnp.zeros((lane - 4,), jnp.float32)]).reshape(1, lane)
    summed = doubling_sum(doubling_sum(jnp.concatenate([cal_term, scalars], axis=0), "cal"), "tm")
    res_sq, curvature, res_q, q_sq = (summed[rows, k] for k in range(4))
    q_cal_all = summed[:rows].reshape(all_blocks, col_width)

    norm_now = res_sq + jnp.sum(cal_res_all * cal_res_all)
    step_len = norm_now / curvature
    new_src_res = src_res - step_len * q_src
    new_att_res = att_res - step_len * q_att
    new_cal_all = cal_res_all - step_len * q_cal_all
    kept = res_sq - step_len * (2.0 * res_q - step_len * q_sq)
    norm_next = kept + jnp.sum(new_cal_all * new_cal_all)
    ratio = norm_next / norm_now
    new_cal_res = lax.dynamic_slice_in_dim(new_cal_all, lax.axis_index("cal") * blocks, blocks, 0)
    return (
        new_src_res,
        new_att_res,
        new_cal_res,
        new_src_res + ratio * src_dir,
        new_att_res + ratio * att_dir,
        new_cal_res + ratio * cal_dir,
    )


def solution(mesh):
    return jax.shard_map(
        local,
        mesh=mesh,
        in_specs=(
            P(None, ("tm", "cal"), None),
            P(None, ("tm", "cal"), None),
            P(("tm", "cal"), None),
            P(("tm", "cal"), None),
            P(("tm", "cal"), None),
            P(("tm", "cal"), None),
            P(("tm", "cal"), None),
            P(("tm", "cal"), None),
            P(("tm", "cal")),
            P(None, ("tm", "cal")),
            P(None, ("tm", "cal")),
            P("cal", None),
            P(None, ("tm", "cal")),
            P(None, ("tm", "cal")),
            P("cal", None),
        ),
        out_specs=(
            P(None, ("tm", "cal")),
            P(None, ("tm", "cal")),
            P("cal", None),
            P(None, ("tm", "cal")),
            P(None, ("tm", "cal")),
            P("cal", None),
        ),
        check_vma=False,
    )
```

```python
import jax
import jax.numpy as jnp
from jax import lax
from jax.sharding import PartitionSpec as P


EXACT = lax.Precision.HIGHEST


def passed_along(block, axis, distance):
    devices = range(lax.axis_size(axis))
    route = [(i - distance, i) for i in devices if i - distance in devices]
    return lax.ppermute(block, axis, route)


def exchanged(block, axis, distance):
    devices = range(lax.axis_size(axis))
    return lax.ppermute(block, axis, [(i, i ^ distance) for i in devices])


def halving_sum(rows, extra, axis):
    count = lax.axis_size(axis)
    me = lax.axis_index(axis)
    bits = count.bit_length() - 1
    order = [int(format(i, "0%db" % bits)[::-1], 2) if bits else 0 for i in range(count)]
    chunks = rows.reshape(count, rows.shape[0] // count, *rows.shape[1:])
    rows = jnp.concatenate([chunks[k] for k in order], axis=0)
    distance = 1
    while distance < count:
        half = rows.shape[0] // 2
        upper = (me // distance) % 2
        keep = lax.dynamic_slice_in_dim(rows, upper * half, half, 0)
        send = lax.dynamic_slice_in_dim(rows, (1 - upper) * half, half, 0)
        got = exchanged(jnp.concatenate([send, extra], axis=0), axis, distance)
        rows = keep + got[:half]
        extra = extra + got[half:]
        distance *= 2
    return rows, extra


def doubling_sum(rows, axis):
    count = lax.axis_size(axis)
    distance = 1
    while distance < count:
        rows = rows + exchanged(rows, axis, distance)
        distance *= 2
    return rows


def doubling_gather(block, axis):
    count = lax.axis_size(axis)
    me = lax.axis_index(axis)
    distance = 1
    while distance < count:
        other = exchanged(block, axis, distance)
        mine_first = (me // distance) % 2 == 0
        block = jnp.where(
            mine_first,
            jnp.concatenate([block, other], axis=1),
            jnp.concatenate([other, block], axis=1),
        )
        distance *= 2
    return block


def spline(phase):
    rest = 1.0 - phase
    cube = phase * phase * phase
    square = phase * phase
    first = rest * rest * rest / 6.0
    second = (3.0 * cube - 6.0 * square + 4.0) / 6.0
    third = (-3.0 * cube + 3.0 * square + 3.0 * phase + 1.0) / 6.0
    fourth = cube / 6.0
    return (first, second, third, fourth)


def local(
    src_design,
    att_design,
    obs_phase,
    cal_design,
    obs_weight,
    knot_index,
    cal_block,
    cal_column,
    obs_count,
    src_res,
    att_res,
    cal_res,
    src_dir,
    att_dir,
    cal_dir,
):
    knot_count = att_dir.shape[1]
    blocks, col_width = cal_dir.shape
    all_blocks = blocks * lax.axis_size("cal")
    cal_size = all_blocks * col_width
    lane = 128
    rows = cal_size // lane
    src_rows, slots = obs_phase.shape

    cal_both = doubling_gather(jnp.stack([cal_dir, cal_res]), "cal")
    cal_values = cal_both[0]
    cal_res_all = cal_both[1]
    edge_knots = passed_along(att_dir[:, :3], ("tm", "cal"), -1)
    att_ext = jnp.concatenate([att_dir, edge_knots], axis=1)

    live_mask = (lax.broadcasted_iota(jnp.int32, obs_phase.shape, 1) < obs_count[:, None]).astype(
        jnp.float32
    )
    basis = spline(obs_phase)
    local_knot = knot_index - lax.axis_index(("tm", "cal")) * knot_count

    n_obs = src_rows * slots
    flat = lambda a: a.reshape(1, n_obs)

    knot_hot = (flat(local_knot) == lax.broadcasted_iota(jnp.int32, (knot_count, 1), 0)).astype(jnp.float32)

    table = jnp.stack([att_ext[:, m : m + knot_count] for m in range(4)], axis=0).reshape(12, knot_count)
    picked = jnp.dot(table, knot_hot, precision=EXACT).reshape(4, 3, src_rows, slots)
    y_att = jnp.zeros_like(obs_phase)
    for m in range(4):
        y_att = y_att + basis[m] * jnp.sum(att_design * picked[m], axis=0)

    flat_index = flat(cal_block * col_width + cal_column)
    high_hot = (flat_index // lane == lax.broadcasted_iota(jnp.int32, (rows, 1), 0)).astype(jnp.float32)
    low_hot = (flat_index % lane == lax.broadcasted_iota(jnp.int32, (lane, 1), 0)).astype(jnp.float32)
    cal_table = cal_values.reshape(rows, lane)
    row_vals = lax.dot_general(cal_table, high_hot, (((0,), (0,)), ((), ())), precision=EXACT)
    y_cal = cal_design * jnp.sum(row_vals * low_hot, axis=0).reshape(src_rows, slots)

    y_src = jnp.sum(src_design * src_dir[:, :, None], axis=0)
    response = live_mask * (y_src + y_att + y_cal)
    weighted = obs_weight * response
    curv_local = jnp.sum(weighted * response)
    q_src = jnp.sum(src_design * weighted[None], axis=2)

    scaled = att_design * weighted[None]
    spread = jnp.stack([basis[m][None] * scaled for m in range(4)], axis=0).reshape(12, n_obs)
    gathered = lax.dot_general(spread, knot_hot, (((1,), (1,)), ((), ())), precision=EXACT)
    gathered = gathered.reshape(4, 3, knot_count)
    grad_ext = jnp.zeros((3, knot_count + 3), jnp.float32)
    for m in range(4):
        grad_ext = grad_ext + jnp.pad(gathered[m], ((0, 0), (m, 3 - m)))
    incoming = passed_along(grad_ext[:, knot_count:], ("tm", "cal"), 1)
    q_att = jnp.concatenate([grad_ext[:, :3] + incoming, grad_ext[:, 3:knot_count]], axis=1)

    cal_weighted = flat(cal_design * weighted) * low_hot
    cal_term = lax.dot_general(high_hot, cal_weighted, (((1,), (1,)), ((), ())), precision=EXACT)
    res_sq = jnp.sum(src_res * src_res) + jnp.sum(att_res * att_res)
    res_q = jnp.sum(src_res * q_src) + jnp.sum(att_res * q_att)
    q_sq = jnp.sum(q_src * q_src) + jnp.sum(q_att * q_att)
    scalars = jnp.stack([res_sq, curv_local, res_q, q_sq])
    scalars = jnp.concatenate([scalars, jnp.zeros((lane - 4,), jnp.float32)]).reshape(1, lane)
    own_rows, scalars = halving_sum(cal_term, scalars, "cal")
    summed = doubling_sum(jnp.concatenate([own_rows, scalars], axis=0), "tm")
    res_sq, curvature, res_q, q_sq = (summed[-1, k] for k in range(4))
    q_cal = summed[:-1].reshape(blocks, col_width)

    norm_now = res_sq + jnp.sum(cal_res_all * cal_res_all)
    step_len = norm_now / curvature
    new_src_res = src_res - step_len * q_src
    new_att_res = att_res - step_len * q_att
    new_cal_res = cal_res - step_len * q_cal
    kept = res_sq - step_len * (2.0 * res_q - step_len * q_sq)
    cal_next = jnp.broadcast_to(jnp.sum(new_cal_res * new_cal_res), (1, lane))
    norm_next = kept + doubling_sum(cal_next, "cal")[0, 0]
    ratio = norm_next / norm_now
    return (
        new_src_res,
        new_att_res,
        new_cal_res,
        new_src_res + ratio * src_dir,
        new_att_res + ratio * att_dir,
        new_cal_res + ratio * cal_dir,
    )


def solution(mesh):
    return jax.shard_map(
        local,
        mesh=mesh,
        in_specs=(
            P(None, ("tm", "cal"), None),
            P(None, ("tm", "cal"), None),
            P(("tm", "cal"), None),
            P(("tm", "cal"), None),
            P(("tm", "cal"), None),
            P(("tm", "cal"), None),
            P(("tm", "cal"), None),
            P(("tm", "cal"), None),
            P(("tm", "cal")),
            P(None, ("tm", "cal")),
            P(None, ("tm", "cal")),
            P("cal", None),
            P(None, ("tm", "cal")),
            P(None, ("tm", "cal")),
            P("cal", None),
        ),
        out_specs=(
            P(None, ("tm", "cal")),
            P(None, ("tm", "cal")),
            P("cal", None),
            P(None, ("tm", "cal")),
            P(None, ("tm", "cal")),
            P("cal", None),
        ),
        check_vma=False,
    )
```

```python
import jax
import jax.numpy as jnp
from jax import lax
from jax.sharding import PartitionSpec as P


EXACT = lax.Precision.HIGHEST


def passed_along(block, axis, distance):
    devices = range(lax.axis_size(axis))
    route = [(i - distance, i) for i in devices if i - distance in devices]
    return lax.ppermute(block, axis, route)


def exchanged(block, axis, distance):
    devices = range(lax.axis_size(axis))
    return lax.ppermute(block, axis, [(i, i ^ distance) for i in devices])


def halving_sum(rows, extra, axis):
    count = lax.axis_size(axis)
    me = lax.axis_index(axis)
    bits = count.bit_length() - 1
    order = [int(format(i, "0%db" % bits)[::-1], 2) if bits else 0 for i in range(count)]
    chunks = rows.reshape(count, rows.shape[0] // count, *rows.shape[1:])
    rows = jnp.concatenate([chunks[k] for k in order], axis=0)
    distance = 1
    while distance < count:
        half = rows.shape[0] // 2
        upper = (me // distance) % 2
        keep = lax.dynamic_slice_in_dim(rows, upper * half, half, 0)
        send = lax.dynamic_slice_in_dim(rows, (1 - upper) * half, half, 0)
        got = exchanged(jnp.concatenate([send, extra], axis=0), axis, distance)
        rows = keep + got[:half]
        extra = extra + got[half:]
        distance *= 2
    return rows, extra


def doubling_sum(rows, axis):
    count = lax.axis_size(axis)
    distance = 1
    while distance < count:
        rows = rows + exchanged(rows, axis, distance)
        distance *= 2
    return rows


def doubling_gather(block, axis):
    count = lax.axis_size(axis)
    me = lax.axis_index(axis)
    distance = 1
    while distance < count:
        other = exchanged(block, axis, distance)
        mine_first = (me // distance) % 2 == 0
        block = jnp.where(
            mine_first,
            jnp.concatenate([block, other], axis=1),
            jnp.concatenate([other, block], axis=1),
        )
        distance *= 2
    return block


def spline(phase):
    rest = 1.0 - phase
    cube = phase * phase * phase
    square = phase * phase
    first = rest * rest * rest / 6.0
    second = (3.0 * cube - 6.0 * square + 4.0) / 6.0
    third = (-3.0 * cube + 3.0 * square + 3.0 * phase + 1.0) / 6.0
    fourth = cube / 6.0
    return (first, second, third, fourth)


def local(
    src_design,
    att_design,
    obs_phase,
    cal_design,
    obs_weight,
    knot_index,
    cal_block,
    cal_column,
    obs_count,
    src_res,
    att_res,
    cal_res,
    src_dir,
    att_dir,
    cal_dir,
):
    knot_count = att_dir.shape[1]
    blocks, col_width = cal_dir.shape
    all_blocks = blocks * lax.axis_size("cal")
    cal_size = all_blocks * col_width
    lane = 128
    rows = cal_size // lane
    src_rows, slots = obs_phase.shape

    cal_values = doubling_gather(cal_dir[None], "cal")[0]
    first_row = (lax.axis_index("tm") == 0).astype(jnp.float32)
    edge_knots = passed_along(att_dir[:, :3], ("tm", "cal"), -1)
    att_ext = jnp.concatenate([att_dir, edge_knots], axis=1)

    live_mask = (lax.broadcasted_iota(jnp.int32, obs_phase.shape, 1) < obs_count[:, None]).astype(
        jnp.float32
    )
    basis = spline(obs_phase)
    local_knot = knot_index - lax.axis_index(("tm", "cal")) * knot_count

    n_obs = src_rows * slots
    flat = lambda a: a.reshape(1, n_obs)

    knot_hot = (flat(local_knot) == lax.broadcasted_iota(jnp.int32, (knot_count, 1), 0)).astype(jnp.float32)

    table = jnp.stack([att_ext[:, m : m + knot_count] for m in range(4)], axis=0).reshape(12, knot_count)
    picked = jnp.dot(table, knot_hot, precision=EXACT).reshape(4, 3, src_rows, slots)
    y_att = jnp.zeros_like(obs_phase)
    for m in range(4):
        y_att = y_att + basis[m] * jnp.sum(att_design * picked[m], axis=0)

    flat_index = flat(cal_block * col_width + cal_column)
    high_hot = (flat_index // lane == lax.broadcasted_iota(jnp.int32, (rows, 1), 0)).astype(jnp.float32)
    low_hot = (flat_index % lane == lax.broadcasted_iota(jnp.int32, (lane, 1), 0)).astype(jnp.float32)
    cal_table = cal_values.reshape(rows, lane)
    row_vals = lax.dot_general(cal_table, high_hot, (((0,), (0,)), ((), ())), precision=EXACT)
    y_cal = cal_design * jnp.sum(row_vals * low_hot, axis=0).reshape(src_rows, slots)

    y_src = jnp.sum(src_design * src_dir[:, :, None], axis=0)
    response = live_mask * (y_src + y_att + y_cal)
    weighted = obs_weight * response
    curv_local = jnp.sum(weighted * response)
    q_src = jnp.sum(src_design * weighted[None], axis=2)

    scaled = att_design * weighted[None]
    spread = jnp.stack([basis[m][None] * scaled for m in range(4)], axis=0).reshape(12, n_obs)
    gathered = lax.dot_general(spread, knot_hot, (((1,), (1,)), ((), ())), precision=EXACT)
    gathered = gathered.reshape(4, 3, knot_count)
    grad_ext = jnp.zeros((3, knot_count + 3), jnp.float32)
    for m in range(4):
        grad_ext = grad_ext + jnp.pad(gathered[m], ((0, 0), (m, 3 - m)))
    incoming = passed_along(grad_ext[:, knot_count:], ("tm", "cal"), 1)
    q_att = jnp.concatenate([grad_ext[:, :3] + incoming, grad_ext[:, 3:knot_count]], axis=1)

    cal_weighted = flat(cal_design * weighted) * low_hot
    cal_term = lax.dot_general(high_hot, cal_weighted, (((1,), (1,)), ((), ())), precision=EXACT)
    res_sq = jnp.sum(src_res * src_res) + jnp.sum(att_res * att_res)
    cal_sq = first_row * jnp.sum(cal_res * cal_res)
    res_q = jnp.sum(src_res * q_src) + jnp.sum(att_res * q_att)
    q_sq = jnp.sum(q_src * q_src) + jnp.sum(q_att * q_att)
    scalars = jnp.stack([res_sq, curv_local, res_q, q_sq, cal_sq])
    scalars = jnp.concatenate([scalars, jnp.zeros((lane - 5,), jnp.float32)]).reshape(1, lane)
    own_rows, scalars = halving_sum(cal_term, scalars, "cal")
    summed = doubling_sum(jnp.concatenate([own_rows, scalars], axis=0), "tm")
    res_sq, curvature, res_q, q_sq, cal_sq = (summed[-1, k] for k in range(5))
    q_cal = summed[:-1].reshape(blocks, col_width)

    norm_now = res_sq + cal_sq
    step_len = norm_now / curvature
    new_src_res = src_res - step_len * q_src
    new_att_res = att_res - step_len * q_att
    new_cal_res = cal_res - step_len * q_cal
    kept = res_sq - step_len * (2.0 * res_q - step_len * q_sq)
    cal_next = jnp.broadcast_to(jnp.sum(new_cal_res * new_cal_res), (1, lane))
    norm_next = kept + doubling_sum(cal_next, "cal")[0, 0]
    ratio = norm_next / norm_now
    return (
        new_src_res,
        new_att_res,
        new_cal_res,
        new_src_res + ratio * src_dir,
        new_att_res + ratio * att_dir,
        new_cal_res + ratio * cal_dir,
    )


def solution(mesh):
    return jax.shard_map(
        local,
        mesh=mesh,
        in_specs=(
            P(None, ("tm", "cal"), None),
            P(None, ("tm", "cal"), None),
            P(("tm", "cal"), None),
            P(("tm", "cal"), None),
            P(("tm", "cal"), None),
            P(("tm", "cal"), None),
            P(("tm", "cal"), None),
            P(("tm", "cal"), None),
            P(("tm", "cal")),
            P(None, ("tm", "cal")),
            P(None, ("tm", "cal")),
            P("cal", None),
            P(None, ("tm", "cal")),
            P(None, ("tm", "cal")),
            P("cal", None),
        ),
        out_specs=(
            P(None, ("tm", "cal")),
            P(None, ("tm", "cal")),
            P("cal", None),
            P(None, ("tm", "cal")),
            P(None, ("tm", "cal")),
            P("cal", None),
        ),
        check_vma=False,
    )
```

```python
import jax
import jax.numpy as jnp
from jax import lax
from jax.sharding import PartitionSpec as P


ONE_HOT_PRECISION = lax.Precision.HIGH


def passed_along(block, axis, distance):
    devices = range(lax.axis_size(axis))
    route = [(i - distance, i) for i in devices if i - distance in devices]
    return lax.ppermute(block, axis, route)


def exchanged(block, axis, distance):
    devices = range(lax.axis_size(axis))
    return lax.ppermute(block, axis, [(i, i ^ distance) for i in devices])


def halving_sum(rows, extra, axis):
    count = lax.axis_size(axis)
    me = lax.axis_index(axis)
    bits = count.bit_length() - 1
    order = [int(format(i, "0%db" % bits)[::-1], 2) if bits else 0 for i in range(count)]
    chunks = rows.reshape(count, rows.shape[0] // count, *rows.shape[1:])
    rows = jnp.concatenate([chunks[k] for k in order], axis=0)
    distance = 1
    while distance < count:
        half = rows.shape[0] // 2
        upper = (me // distance) % 2
        keep = lax.dynamic_slice_in_dim(rows, upper * half, half, 0)
        send = lax.dynamic_slice_in_dim(rows, (1 - upper) * half, half, 0)
        got = exchanged(jnp.concatenate([send, extra], axis=0), axis, distance)
        rows = keep + got[:half]
        extra = extra + got[half:]
        distance *= 2
    return rows, extra


def doubling_sum(rows, axis):
    count = lax.axis_size(axis)
    distance = 1
    while distance < count:
        rows = rows + exchanged(rows, axis, distance)
        distance *= 2
    return rows


def doubling_gather(block, axis):
    count = lax.axis_size(axis)
    me = lax.axis_index(axis)
    distance = 1
    while distance < count:
        other = exchanged(block, axis, distance)
        mine_first = (me // distance) % 2 == 0
        block = jnp.where(
            mine_first,
            jnp.concatenate([block, other], axis=1),
            jnp.concatenate([other, block], axis=1),
        )
        distance *= 2
    return block


def spline(phase):
    rest = 1.0 - phase
    cube = phase * phase * phase
    square = phase * phase
    first = rest * rest * rest / 6.0
    second = (3.0 * cube - 6.0 * square + 4.0) / 6.0
    third = (-3.0 * cube + 3.0 * square + 3.0 * phase + 1.0) / 6.0
    fourth = cube / 6.0
    return (first, second, third, fourth)


def local(
    src_design,
    att_design,
    obs_phase,
    cal_design,
    obs_weight,
    knot_index,
    cal_block,
    cal_column,
    obs_count,
    src_res,
    att_res,
    cal_res,
    src_dir,
    att_dir,
    cal_dir,
):
    knot_count = att_dir.shape[1]
    blocks, col_width = cal_dir.shape
    all_blocks = blocks * lax.axis_size("cal")
    cal_size = all_blocks * col_width
    lane = 128
    rows = cal_size // lane
    src_rows, slots = obs_phase.shape

    cal_values = doubling_gather(cal_dir[None], "cal")[0]
    first_row = (lax.axis_index("tm") == 0).astype(jnp.float32)
    edge_knots = passed_along(att_dir[:, :3], ("tm", "cal"), -1)
    att_ext = jnp.concatenate([att_dir, edge_knots], axis=1)

    live_mask = (lax.broadcasted_iota(jnp.int32, obs_phase.shape, 1) < obs_count[:, None]).astype(
        jnp.float32
    )
    basis = spline(obs_phase)
    local_knot = knot_index - lax.axis_index(("tm", "cal")) * knot_count

    n_obs = src_rows * slots
    flat = lambda a: a.reshape(1, n_obs)

    knot_hot = (flat(local_knot) == lax.broadcasted_iota(jnp.int32, (knot_count, 1), 0)).astype(jnp.float32)

    table = jnp.stack([att_ext[:, m : m + knot_count] for m in range(4)], axis=0).reshape(12, knot_count)
    picked = jnp.dot(table, knot_hot, precision=ONE_HOT_PRECISION).reshape(4, 3, src_rows, slots)
    y_att = jnp.zeros_like(obs_phase)
    for m in range(4):
        y_att = y_att + basis[m] * jnp.sum(att_design * picked[m], axis=0)

    flat_index = flat(cal_block * col_width + cal_column)
    high_hot = (flat_index // lane == lax.broadcasted_iota(jnp.int32, (rows, 1), 0)).astype(jnp.float32)
    low_hot = (flat_index % lane == lax.broadcasted_iota(jnp.int32, (lane, 1), 0)).astype(jnp.float32)
    cal_table = cal_values.reshape(rows, lane)
    row_vals = lax.dot_general(cal_table, high_hot, (((0,), (0,)), ((), ())), precision=ONE_HOT_PRECISION)
    y_cal = cal_design * jnp.sum(row_vals * low_hot, axis=0).reshape(src_rows, slots)

    y_src = jnp.sum(src_design * src_dir[:, :, None], axis=0)
    response = live_mask * (y_src + y_att + y_cal)
    weighted = obs_weight * response
    curv_local = jnp.sum(weighted * response)
    q_src = jnp.sum(src_design * weighted[None], axis=2)

    scaled = att_design * weighted[None]
    spread = jnp.stack([basis[m][None] * scaled for m in range(4)], axis=0).reshape(12, n_obs)
    gathered = lax.dot_general(spread, knot_hot, (((1,), (1,)), ((), ())), precision=ONE_HOT_PRECISION)
    gathered = gathered.reshape(4, 3, knot_count)
    grad_ext = jnp.zeros((3, knot_count + 3), jnp.float32)
    for m in range(4):
        grad_ext = grad_ext + jnp.pad(gathered[m], ((0, 0), (m, 3 - m)))
    incoming = passed_along(grad_ext[:, knot_count:], ("tm", "cal"), 1)
    q_att = jnp.concatenate([grad_ext[:, :3] + incoming, grad_ext[:, 3:knot_count]], axis=1)

    cal_weighted = flat(cal_design * weighted) * low_hot
    cal_term = lax.dot_general(high_hot, cal_weighted, (((1,), (1,)), ((), ())), precision=ONE_HOT_PRECISION)
    res_sq = jnp.sum(src_res * src_res) + jnp.sum(att_res * att_res)
    cal_sq = first_row * jnp.sum(cal_res * cal_res)
    res_q = jnp.sum(src_res * q_src) + jnp.sum(att_res * q_att)
    q_sq = jnp.sum(q_src * q_src) + jnp.sum(q_att * q_att)
    scalars = jnp.stack([res_sq, curv_local, res_q, q_sq, cal_sq])
    scalars = jnp.concatenate([scalars, jnp.zeros((lane - 5,), jnp.float32)]).reshape(1, lane)
    own_rows, scalars = halving_sum(cal_term, scalars, "cal")
    summed = doubling_sum(jnp.concatenate([own_rows, scalars], axis=0), "tm")
    res_sq, curvature, res_q, q_sq, cal_sq = (summed[-1, k] for k in range(5))
    q_cal = summed[:-1].reshape(blocks, col_width)

    norm_now = res_sq + cal_sq
    step_len = norm_now / curvature
    new_src_res = src_res - step_len * q_src
    new_att_res = att_res - step_len * q_att
    new_cal_res = cal_res - step_len * q_cal
    kept = res_sq - step_len * (2.0 * res_q - step_len * q_sq)
    cal_next = jnp.broadcast_to(jnp.sum(new_cal_res * new_cal_res), (1, lane))
    norm_next = kept + doubling_sum(cal_next, "cal")[0, 0]
    ratio = norm_next / norm_now
    return (
        new_src_res,
        new_att_res,
        new_cal_res,
        new_src_res + ratio * src_dir,
        new_att_res + ratio * att_dir,
        new_cal_res + ratio * cal_dir,
    )


def solution(mesh):
    return jax.shard_map(
        local,
        mesh=mesh,
        in_specs=(
            P(None, ("tm", "cal"), None),
            P(None, ("tm", "cal"), None),
            P(("tm", "cal"), None),
            P(("tm", "cal"), None),
            P(("tm", "cal"), None),
            P(("tm", "cal"), None),
            P(("tm", "cal"), None),
            P(("tm", "cal"), None),
            P(("tm", "cal")),
            P(None, ("tm", "cal")),
            P(None, ("tm", "cal")),
            P("cal", None),
            P(None, ("tm", "cal")),
            P(None, ("tm", "cal")),
            P("cal", None),
        ),
        out_specs=(
            P(None, ("tm", "cal")),
            P(None, ("tm", "cal")),
            P("cal", None),
            P(None, ("tm", "cal")),
            P(None, ("tm", "cal")),
            P("cal", None),
        ),
        check_vma=False,
    )
```

```python
import jax
import jax.numpy as jnp
from jax import lax
from jax.sharding import PartitionSpec as P


ONE_HOT_PRECISION = lax.Precision.HIGH


def passed_along(block, axis, distance):
    devices = range(lax.axis_size(axis))
    route = [(i - distance, i) for i in devices if i - distance in devices]
    return lax.ppermute(block, axis, route)


def exchanged(block, axis, distance):
    devices = range(lax.axis_size(axis))
    return lax.ppermute(block, axis, [(i, i ^ distance) for i in devices])


def halving_sum(rows, extra, axis):
    count = lax.axis_size(axis)
    me = lax.axis_index(axis)
    bits = count.bit_length() - 1
    order = [int(format(i, "0%db" % bits)[::-1], 2) if bits else 0 for i in range(count)]
    chunks = rows.reshape(count, rows.shape[0] // count, *rows.shape[1:])
    rows = jnp.concatenate([chunks[k] for k in order], axis=0)
    distance = 1
    while distance < count:
        half = rows.shape[0] // 2
        upper = (me // distance) % 2
        keep = lax.dynamic_slice_in_dim(rows, upper * half, half, 0)
        send = lax.dynamic_slice_in_dim(rows, (1 - upper) * half, half, 0)
        got = exchanged(jnp.concatenate([send, extra], axis=0), axis, distance)
        rows = keep + got[:half]
        extra = extra + got[half:]
        distance *= 2
    return rows, extra


def doubling_sum(rows, axis):
    count = lax.axis_size(axis)
    distance = 1
    while distance < count:
        rows = rows + exchanged(rows, axis, distance)
        distance *= 2
    return rows


def doubling_gather(block, axis):
    count = lax.axis_size(axis)
    me = lax.axis_index(axis)
    distance = 1
    while distance < count:
        other = exchanged(block, axis, distance)
        mine_first = (me // distance) % 2 == 0
        block = jnp.where(
            mine_first,
            jnp.concatenate([block, other], axis=1),
            jnp.concatenate([other, block], axis=1),
        )
        distance *= 2
    return block


def spline(phase):
    rest = 1.0 - phase
    cube = phase * phase * phase
    square = phase * phase
    first = rest * rest * rest / 6.0
    second = (3.0 * cube - 6.0 * square + 4.0) / 6.0
    third = (-3.0 * cube + 3.0 * square + 3.0 * phase + 1.0) / 6.0
    fourth = cube / 6.0
    return (first, second, third, fourth)


def local(
    src_design,
    att_design,
    obs_phase,
    cal_design,
    obs_weight,
    knot_index,
    cal_block,
    cal_column,
    obs_count,
    src_res,
    att_res,
    cal_res,
    src_dir,
    att_dir,
    cal_dir,
):
    knot_count = att_dir.shape[1]
    blocks, col_width = cal_dir.shape
    all_blocks = blocks * lax.axis_size("cal")
    cal_size = all_blocks * col_width
    lane = 128
    rows = cal_size // lane
    src_rows, slots = obs_phase.shape

    cal_values = doubling_gather(cal_dir[None], "cal")[0]
    first_row = (lax.axis_index("tm") == 0).astype(jnp.float32)
    edge_knots = passed_along(att_dir[:, :3], ("tm", "cal"), -1)
    att_ext = jnp.concatenate([att_dir, edge_knots], axis=1)

    live_mask = (lax.broadcasted_iota(jnp.int32, obs_phase.shape, 1) < obs_count[:, None]).astype(
        jnp.float32
    )
    basis = spline(obs_phase)
    local_knot = knot_index - lax.axis_index(("tm", "cal")) * knot_count

    n_obs = src_rows * slots
    flat = lambda a: a.reshape(1, n_obs)

    knot_hot = (flat(local_knot) == lax.broadcasted_iota(jnp.int32, (knot_count, 1), 0)).astype(jnp.float32)

    table = jnp.stack([att_ext[:, m : m + knot_count] for m in range(4)], axis=0).reshape(12, knot_count)
    picked = jnp.dot(table, knot_hot, precision=ONE_HOT_PRECISION).reshape(4, 3, src_rows, slots)
    y_att = jnp.zeros_like(obs_phase)
    for m in range(4):
        y_att = y_att + basis[m] * jnp.sum(att_design * picked[m], axis=0)

    flat_index = flat(cal_block * col_width + cal_column)
    high_hot = (flat_index // lane == lax.broadcasted_iota(jnp.int32, (rows, 1), 0)).astype(jnp.float32)
    low_hot = (flat_index % lane == lax.broadcasted_iota(jnp.int32, (lane, 1), 0)).astype(jnp.float32)
    cal_table = cal_values.reshape(rows, lane)
    row_vals = lax.dot_general(cal_table, high_hot, (((0,), (0,)), ((), ())), precision=ONE_HOT_PRECISION)
    y_cal = cal_design * jnp.sum(row_vals * low_hot, axis=0).reshape(src_rows, slots)

    y_src = jnp.sum(src_design * src_dir[:, :, None], axis=0)
    response = live_mask * (y_src + y_att + y_cal)
    weighted = obs_weight * response
    curv_local = jnp.sum(weighted * response)
    q_src = jnp.sum(src_design * weighted[None], axis=2)

    scaled = att_design * weighted[None]
    spread = jnp.stack([basis[m][None] * scaled for m in range(4)], axis=0).reshape(12, n_obs)
    gathered = lax.dot_general(spread, knot_hot, (((1,), (1,)), ((), ())), precision=ONE_HOT_PRECISION)
    gathered = gathered.reshape(4, 3, knot_count)
    grad_ext = jnp.zeros((3, knot_count + 3), jnp.float32)
    for m in range(4):
        grad_ext = grad_ext + jnp.pad(gathered[m], ((0, 0), (m, 3 - m)))
    incoming = passed_along(grad_ext[:, knot_count:], ("tm", "cal"), 1)
    q_att = jnp.concatenate([grad_ext[:, :3] + incoming, grad_ext[:, 3:knot_count]], axis=1)

    cal_weighted = flat(cal_design * weighted) * low_hot
    row_start = lax.broadcasted_iota(jnp.int32, (rows, 1), 0) * lane
    high_range = ((flat_index >= row_start) & (flat_index < row_start + lane)).astype(jnp.float32)
    cal_term = lax.dot_general(high_range, cal_weighted, (((1,), (1,)), ((), ())), precision=ONE_HOT_PRECISION)
    res_sq = jnp.sum(src_res * src_res) + jnp.sum(att_res * att_res)
    cal_sq = first_row * jnp.sum(cal_res * cal_res)
    res_q = jnp.sum(src_res * q_src) + jnp.sum(att_res * q_att)
    q_sq = jnp.sum(q_src * q_src) + jnp.sum(q_att * q_att)
    scalars = jnp.stack([res_sq, curv_local, res_q, q_sq, cal_sq])
    scalars = jnp.concatenate([scalars, jnp.zeros((lane - 5,), jnp.float32)]).reshape(1, lane)
    own_rows, scalars = halving_sum(cal_term, scalars, "cal")
    summed = doubling_sum(jnp.concatenate([own_rows, scalars], axis=0), "tm")
    res_sq, curvature, res_q, q_sq, cal_sq = (summed[-1, k] for k in range(5))
    q_cal = summed[:-1].reshape(blocks, col_width)

    norm_now = res_sq + cal_sq
    step_len = norm_now / curvature
    new_src_res = src_res - step_len * q_src
    new_att_res = att_res - step_len * q_att
    new_cal_res = cal_res - step_len * q_cal
    kept = res_sq - step_len * (2.0 * res_q - step_len * q_sq)
    cal_next = jnp.broadcast_to(jnp.sum(new_cal_res * new_cal_res), (1, lane))
    norm_next = kept + doubling_sum(cal_next, "cal")[0, 0]
    ratio = norm_next / norm_now
    return (
        new_src_res,
        new_att_res,
        new_cal_res,
        new_src_res + ratio * src_dir,
        new_att_res + ratio * att_dir,
        new_cal_res + ratio * cal_dir,
    )


def solution(mesh):
    return jax.shard_map(
        local,
        mesh=mesh,
        in_specs=(
            P(None, ("tm", "cal"), None),
            P(None, ("tm", "cal"), None),
            P(("tm", "cal"), None),
            P(("tm", "cal"), None),
            P(("tm", "cal"), None),
            P(("tm", "cal"), None),
            P(("tm", "cal"), None),
            P(("tm", "cal"), None),
            P(("tm", "cal")),
            P(None, ("tm", "cal")),
            P(None, ("tm", "cal")),
            P("cal", None),
            P(None, ("tm", "cal")),
            P(None, ("tm", "cal")),
            P("cal", None),
        ),
        out_specs=(
            P(None, ("tm", "cal")),
            P(None, ("tm", "cal")),
            P("cal", None),
            P(None, ("tm", "cal")),
            P(None, ("tm", "cal")),
            P("cal", None),
        ),
        check_vma=False,
    )
```

```python
import jax
import jax.numpy as jnp
from jax import lax
from jax.sharding import PartitionSpec as P


ONE_HOT_PRECISION = lax.Precision.HIGH


def passed_along(block, axis, distance):
    devices = range(lax.axis_size(axis))
    route = [(i - distance, i) for i in devices if i - distance in devices]
    return lax.ppermute(block, axis, route)


def exchanged(block, axis, distance):
    devices = range(lax.axis_size(axis))
    return lax.ppermute(block, axis, [(i, i ^ distance) for i in devices])


def halving_sum(rows, extra, axis):
    count = lax.axis_size(axis)
    me = lax.axis_index(axis)
    bits = count.bit_length() - 1
    order = [int(format(i, "0%db" % bits)[::-1], 2) if bits else 0 for i in range(count)]
    chunks = rows.reshape(count, rows.shape[0] // count, *rows.shape[1:])
    rows = jnp.concatenate([chunks[k] for k in order], axis=0)
    distance = 1
    while distance < count:
        half = rows.shape[0] // 2
        upper = (me // distance) % 2
        keep = lax.dynamic_slice_in_dim(rows, upper * half, half, 0)
        send = lax.dynamic_slice_in_dim(rows, (1 - upper) * half, half, 0)
        got = exchanged(jnp.concatenate([send, extra], axis=0), axis, distance)
        rows = keep + got[:half]
        extra = extra + got[half:]
        distance *= 2
    return rows, extra


def doubling_sum(rows, axis):
    count = lax.axis_size(axis)
    distance = 1
    while distance < count:
        rows = rows + exchanged(rows, axis, distance)
        distance *= 2
    return rows


def doubling_gather(block, axis):
    count = lax.axis_size(axis)
    me = lax.axis_index(axis)
    distance = 1
    while distance < count:
        other = exchanged(block, axis, distance)
        mine_first = (me // distance) % 2 == 0
        block = jnp.where(
            mine_first,
            jnp.concatenate([block, other], axis=1),
            jnp.concatenate([other, block], axis=1),
        )
        distance *= 2
    return block


def spline(phase):
    rest = 1.0 - phase
    cube = phase * phase * phase
    square = phase * phase
    first = rest * rest * rest / 6.0
    second = (3.0 * cube - 6.0 * square + 4.0) / 6.0
    third = (-3.0 * cube + 3.0 * square + 3.0 * phase + 1.0) / 6.0
    fourth = cube / 6.0
    return (first, second, third, fourth)


def local(
    src_design,
    att_design,
    obs_phase,
    cal_design,
    obs_weight,
    knot_index,
    cal_block,
    cal_column,
    obs_count,
    src_res,
    att_res,
    cal_res,
    src_dir,
    att_dir,
    cal_dir,
):
    knot_count = att_dir.shape[1]
    blocks, col_width = cal_dir.shape
    all_blocks = blocks * lax.axis_size("cal")
    cal_size = all_blocks * col_width
    lane = 128
    rows = cal_size // lane
    src_rows, slots = obs_phase.shape

    cal_both = doubling_gather(jnp.stack([cal_dir, cal_res]), "cal")
    cal_values = cal_both[0]
    first_row = (lax.axis_index("tm") == 0).astype(jnp.float32)
    edge_knots = passed_along(att_dir[:, :3], ("tm", "cal"), -1)
    att_ext = jnp.concatenate([att_dir, edge_knots], axis=1)

    live_mask = (lax.broadcasted_iota(jnp.int32, obs_phase.shape, 1) < obs_count[:, None]).astype(
        jnp.float32
    )
    basis = spline(obs_phase)
    local_knot = knot_index - lax.axis_index(("tm", "cal")) * knot_count

    n_obs = src_rows * slots
    flat = lambda a: a.reshape(1, n_obs)

    knot_hot = (flat(local_knot) == lax.broadcasted_iota(jnp.int32, (knot_count, 1), 0)).astype(jnp.float32)

    table = jnp.stack([att_ext[:, m : m + knot_count] for m in range(4)], axis=0).reshape(12, knot_count)
    picked = jnp.dot(table, knot_hot, precision=ONE_HOT_PRECISION).reshape(4, 3, src_rows, slots)
    y_att = jnp.zeros_like(obs_phase)
    for m in range(4):
        y_att = y_att + basis[m] * jnp.sum(att_design * picked[m], axis=0)

    flat_index = flat(cal_block * col_width + cal_column)
    high_hot = (flat_index // lane == lax.broadcasted_iota(jnp.int32, (rows, 1), 0)).astype(jnp.float32)
    low_hot = (flat_index % lane == lax.broadcasted_iota(jnp.int32, (lane, 1), 0)).astype(jnp.float32)
    cal_table = cal_values.reshape(rows, lane)
    row_vals = lax.dot_general(cal_table, high_hot, (((0,), (0,)), ((), ())), precision=ONE_HOT_PRECISION)
    y_cal = cal_design * jnp.sum(row_vals * low_hot, axis=0).reshape(src_rows, slots)

    y_src = jnp.sum(src_design * src_dir[:, :, None], axis=0)
    response = live_mask * (y_src + y_att + y_cal)
    weighted = obs_weight * response
    curv_local = jnp.sum(weighted * response)
    q_src = jnp.sum(src_design * weighted[None], axis=2)

    scaled = att_design * weighted[None]
    spread = jnp.stack([basis[m][None] * scaled for m in range(4)], axis=0).reshape(12, n_obs)
    gathered = lax.dot_general(spread, knot_hot, (((1,), (1,)), ((), ())), precision=ONE_HOT_PRECISION)
    gathered = gathered.reshape(4, 3, knot_count)
    grad_ext = jnp.zeros((3, knot_count + 3), jnp.float32)
    for m in range(4):
        grad_ext = grad_ext + jnp.pad(gathered[m], ((0, 0), (m, 3 - m)))
    incoming = passed_along(grad_ext[:, knot_count:], ("tm", "cal"), 1)
    q_att = jnp.concatenate([grad_ext[:, :3] + incoming, grad_ext[:, 3:knot_count]], axis=1)

    cal_weighted = flat(cal_design * weighted) * low_hot
    cal_term = lax.dot_general(high_hot, cal_weighted, (((1,), (1,)), ((), ())), precision=ONE_HOT_PRECISION)
    res_sq = jnp.sum(src_res * src_res) + jnp.sum(att_res * att_res)
    cal_sq = first_row * jnp.sum(cal_res * cal_res)
    res_q = jnp.sum(src_res * q_src) + jnp.sum(att_res * q_att)
    q_sq = jnp.sum(q_src * q_src) + jnp.sum(q_att * q_att)
    scalars = jnp.stack([res_sq, curv_local, res_q, q_sq, cal_sq])
    scalars = jnp.concatenate([scalars, jnp.zeros((lane - 5,), jnp.float32)]).reshape(1, lane)
    cal_count = lax.axis_size("cal")
    cal_me = lax.axis_index("cal")
    parity = cal_me % 2
    share = rows // cal_count
    chunks = cal_term.reshape(cal_count // 2, 2, share, lane)
    keep = lax.dynamic_index_in_dim(chunks, parity, axis=1, keepdims=False).reshape(-1, lane)
    send = lax.dynamic_index_in_dim(chunks, 1 - parity, axis=1, keepdims=False).reshape(-1, lane)
    got = exchanged(jnp.concatenate([send, scalars], axis=0), "cal", 1)
    summed = jnp.concatenate([keep + got[:-1], scalars + got[-1:]], axis=0)
    distance = 2
    while distance < cal_count:
        summed = summed + exchanged(summed, "cal", distance)
        distance *= 2
    summed = doubling_sum(summed, "tm")
    res_sq, curvature, res_q, q_sq, cal_sq = (summed[-1, k] for k in range(5))
    q_kept = summed[:-1].reshape(cal_count // 2, blocks * col_width)

    norm_now = res_sq + cal_sq
    step_len = norm_now / curvature
    new_src_res = src_res - step_len * q_src
    new_att_res = att_res - step_len * q_att
    res_kept = cal_both[1].reshape(cal_count // 2, 2, blocks * col_width)
    res_kept = lax.dynamic_index_in_dim(res_kept, parity, axis=1, keepdims=False)
    new_kept = res_kept - step_len * q_kept
    new_cal_res = lax.dynamic_index_in_dim(new_kept, cal_me // 2, axis=0, keepdims=False)
    new_cal_res = new_cal_res.reshape(blocks, col_width)
    kept = res_sq - step_len * (2.0 * res_q - step_len * q_sq)
    cal_next = jnp.broadcast_to(jnp.sum(new_kept * new_kept), (1, lane))
    norm_next = kept + (cal_next + exchanged(cal_next, "cal", 1))[0, 0]
    ratio = norm_next / norm_now
    return (
        new_src_res,
        new_att_res,
        new_cal_res,
        new_src_res + ratio * src_dir,
        new_att_res + ratio * att_dir,
        new_cal_res + ratio * cal_dir,
    )


def solution(mesh):
    return jax.shard_map(
        local,
        mesh=mesh,
        in_specs=(
            P(None, ("tm", "cal"), None),
            P(None, ("tm", "cal"), None),
            P(("tm", "cal"), None),
            P(("tm", "cal"), None),
            P(("tm", "cal"), None),
            P(("tm", "cal"), None),
            P(("tm", "cal"), None),
            P(("tm", "cal"), None),
            P(("tm", "cal")),
            P(None, ("tm", "cal")),
            P(None, ("tm", "cal")),
            P("cal", None),
            P(None, ("tm", "cal")),
            P(None, ("tm", "cal")),
            P("cal", None),
        ),
        out_specs=(
            P(None, ("tm", "cal")),
            P(None, ("tm", "cal")),
            P("cal", None),
            P(None, ("tm", "cal")),
            P(None, ("tm", "cal")),
            P("cal", None),
        ),
        check_vma=False,
    )
```

```python
import jax
import jax.numpy as jnp
from jax import lax
from jax.sharding import PartitionSpec as P


ONE_HOT_PRECISION = lax.Precision.HIGH


def passed_along(block, axis, distance):
    devices = range(lax.axis_size(axis))
    route = [(i - distance, i) for i in devices if i - distance in devices]
    return lax.ppermute(block, axis, route)


def exchanged(block, axis, distance):
    devices = range(lax.axis_size(axis))
    return lax.ppermute(block, axis, [(i, i ^ distance) for i in devices])


def halving_sum(rows, extra, axis):
    count = lax.axis_size(axis)
    me = lax.axis_index(axis)
    bits = count.bit_length() - 1
    order = [int(format(i, "0%db" % bits)[::-1], 2) if bits else 0 for i in range(count)]
    chunks = rows.reshape(count, rows.shape[0] // count, *rows.shape[1:])
    rows = jnp.concatenate([chunks[k] for k in order], axis=0)
    distance = 1
    while distance < count:
        half = rows.shape[0] // 2
        upper = (me // distance) % 2
        keep = lax.dynamic_slice_in_dim(rows, upper * half, half, 0)
        send = lax.dynamic_slice_in_dim(rows, (1 - upper) * half, half, 0)
        got = exchanged(jnp.concatenate([send, extra], axis=0), axis, distance)
        rows = keep + got[:half]
        extra = extra + got[half:]
        distance *= 2
    return rows, extra


def doubling_sum(rows, axis):
    count = lax.axis_size(axis)
    distance = 1
    while distance < count:
        rows = rows + exchanged(rows, axis, distance)
        distance *= 2
    return rows


def doubling_gather(block, axis):
    count = lax.axis_size(axis)
    me = lax.axis_index(axis)
    distance = 1
    while distance < count:
        other = exchanged(block, axis, distance)
        mine_first = (me // distance) % 2 == 0
        block = jnp.where(
            mine_first,
            jnp.concatenate([block, other], axis=1),
            jnp.concatenate([other, block], axis=1),
        )
        distance *= 2
    return block


def spline(phase):
    rest = 1.0 - phase
    cube = phase * phase * phase
    square = phase * phase
    first = rest * rest * rest / 6.0
    second = (3.0 * cube - 6.0 * square + 4.0) / 6.0
    third = (-3.0 * cube + 3.0 * square + 3.0 * phase + 1.0) / 6.0
    fourth = cube / 6.0
    return (first, second, third, fourth)


def local(
    src_design,
    att_design,
    obs_phase,
    cal_design,
    obs_weight,
    knot_index,
    cal_block,
    cal_column,
    obs_count,
    src_res,
    att_res,
    cal_res,
    src_dir,
    att_dir,
    cal_dir,
):
    knot_count = att_dir.shape[1]
    blocks, col_width = cal_dir.shape
    all_blocks = blocks * lax.axis_size("cal")
    cal_size = all_blocks * col_width
    lane = 128
    rows = cal_size // lane
    src_rows, slots = obs_phase.shape

    cal_values = doubling_gather(cal_dir[None], "cal")[0]
    first_row = (lax.axis_index("tm") == 0).astype(jnp.float32)
    edge_both = passed_along(jnp.stack([att_dir[:, :3], att_res[:, :3]]), ("tm", "cal"), -1)
    att_ext = jnp.concatenate([att_dir, edge_both[0]], axis=1)
    next_res = edge_both[1]

    live_mask = (lax.broadcasted_iota(jnp.int32, obs_phase.shape, 1) < obs_count[:, None]).astype(
        jnp.float32
    )
    basis = spline(obs_phase)
    local_knot = knot_index - lax.axis_index(("tm", "cal")) * knot_count

    n_obs = src_rows * slots
    flat = lambda a: a.reshape(1, n_obs)

    knot_hot = (flat(local_knot) == lax.broadcasted_iota(jnp.int32, (knot_count, 1), 0)).astype(jnp.float32)

    table = jnp.stack([att_ext[:, m : m + knot_count] for m in range(4)], axis=0).reshape(12, knot_count)
    picked = jnp.dot(table, knot_hot, precision=ONE_HOT_PRECISION).reshape(4, 3, src_rows, slots)
    y_att = jnp.zeros_like(obs_phase)
    for m in range(4):
        y_att = y_att + basis[m] * jnp.sum(att_design * picked[m], axis=0)

    flat_index = flat(cal_block * col_width + cal_column)
    high_hot = (flat_index // lane == lax.broadcasted_iota(jnp.int32, (rows, 1), 0)).astype(jnp.float32)
    low_hot = (flat_index % lane == lax.broadcasted_iota(jnp.int32, (lane, 1), 0)).astype(jnp.float32)
    cal_table = cal_values.reshape(rows, lane)
    row_vals = lax.dot_general(cal_table, high_hot, (((0,), (0,)), ((), ())), precision=ONE_HOT_PRECISION)
    y_cal = cal_design * jnp.sum(row_vals * low_hot, axis=0).reshape(src_rows, slots)

    y_src = jnp.sum(src_design * src_dir[:, :, None], axis=0)
    response = live_mask * (y_src + y_att + y_cal)
    weighted = obs_weight * response
    curv_local = jnp.sum(weighted * response)
    q_src = jnp.sum(src_design * weighted[None], axis=2)

    scaled = att_design * weighted[None]
    spread = jnp.stack([basis[m][None] * scaled for m in range(4)], axis=0).reshape(12, n_obs)
    gathered = lax.dot_general(spread, knot_hot, (((1,), (1,)), ((), ())), precision=ONE_HOT_PRECISION)
    gathered = gathered.reshape(4, 3, knot_count)
    grad_ext = jnp.zeros((3, knot_count + 3), jnp.float32)
    for m in range(4):
        grad_ext = grad_ext + jnp.pad(gathered[m], ((0, 0), (m, 3 - m)))
    own_att = grad_ext[:, :knot_count]
    edge_out = grad_ext[:, knot_count:]

    cal_weighted = flat(cal_design * weighted) * low_hot
    cal_term = lax.dot_general(high_hot, cal_weighted, (((1,), (1,)), ((), ())), precision=ONE_HOT_PRECISION)
    res_sq = jnp.sum(src_res * src_res) + jnp.sum(att_res * att_res)
    cal_sq = first_row * jnp.sum(cal_res * cal_res)
    res_q = jnp.sum(src_res * q_src) + jnp.sum(att_res * own_att) + jnp.sum(next_res * edge_out)
    q_sq = jnp.sum(q_src * q_src) + jnp.sum(own_att * own_att)
    scalars = jnp.stack([res_sq, curv_local, res_q, q_sq, cal_sq])
    scalars = jnp.concatenate([scalars, jnp.zeros((lane - 5,), jnp.float32)]).reshape(1, lane)
    device_count = lax.axis_size(("tm", "cal"))
    device = lax.axis_index(("tm", "cal"))
    slot_rows = -(-device_count * 9 // lane)
    mine = (lax.broadcasted_iota(jnp.int32, (device_count, 1), 0) == device).astype(jnp.float32)

    def slotted(values):
        table = (mine * values.reshape(1, 9)).reshape(-1)
        return jnp.pad(table, (0, slot_rows * lane - device_count * 9)).reshape(slot_rows, lane)

    extra = jnp.concatenate([scalars, slotted(edge_out), slotted(own_att[:, :3])], axis=0)
    own_rows, extra = halving_sum(cal_term, extra, "cal")
    summed = doubling_sum(jnp.concatenate([own_rows, extra], axis=0), "tm")
    res_sq, curvature, res_q, q_sq, cal_sq = (summed[-2 * slot_rows - 1, k] for k in range(5))
    q_cal = summed[: -2 * slot_rows - 1].reshape(blocks, col_width)
    edges = summed[-2 * slot_rows :].reshape(2, -1)[:, : device_count * 9].reshape(2, device_count, 9)
    sent, heads = edges[0, :-1], edges[1, 1:]
    q_sq = q_sq + jnp.sum(sent * sent) + 2.0 * jnp.sum(sent * heads)
    previous = jnp.maximum(device - 1, 0)
    incoming = lax.dynamic_index_in_dim(edges[0], previous, axis=0, keepdims=False).reshape(3, 3)
    incoming = incoming * (device > 0).astype(jnp.float32)
    q_att = jnp.concatenate([own_att[:, :3] + incoming, own_att[:, 3:]], axis=1)

    norm_now = res_sq + cal_sq
    step_len = norm_now / curvature
    new_src_res = src_res - step_len * q_src
    new_att_res = att_res - step_len * q_att
    new_cal_res = cal_res - step_len * q_cal
    kept = res_sq - step_len * (2.0 * res_q - step_len * q_sq)
    cal_next = jnp.broadcast_to(jnp.sum(new_cal_res * new_cal_res), (1, lane))
    norm_next = kept + doubling_sum(cal_next, "cal")[0, 0]
    ratio = norm_next / norm_now
    return (
        new_src_res,
        new_att_res,
        new_cal_res,
        new_src_res + ratio * src_dir,
        new_att_res + ratio * att_dir,
        new_cal_res + ratio * cal_dir,
    )


def solution(mesh):
    return jax.shard_map(
        local,
        mesh=mesh,
        in_specs=(
            P(None, ("tm", "cal"), None),
            P(None, ("tm", "cal"), None),
            P(("tm", "cal"), None),
            P(("tm", "cal"), None),
            P(("tm", "cal"), None),
            P(("tm", "cal"), None),
            P(("tm", "cal"), None),
            P(("tm", "cal"), None),
            P(("tm", "cal")),
            P(None, ("tm", "cal")),
            P(None, ("tm", "cal")),
            P("cal", None),
            P(None, ("tm", "cal")),
            P(None, ("tm", "cal")),
            P("cal", None),
        ),
        out_specs=(
            P(None, ("tm", "cal")),
            P(None, ("tm", "cal")),
            P("cal", None),
            P(None, ("tm", "cal")),
            P(None, ("tm", "cal")),
            P("cal", None),
        ),
        check_vma=False,
    )
```

```python
import jax
import jax.numpy as jnp
from jax import lax
from jax.sharding import PartitionSpec as P


ONE_HOT_PRECISION = lax.Precision.HIGH


def passed_along(block, axis, distance):
    devices = range(lax.axis_size(axis))
    route = [(i - distance, i) for i in devices if i - distance in devices]
    return lax.ppermute(block, axis, route)


def exchanged(block, axis, distance):
    devices = range(lax.axis_size(axis))
    return lax.ppermute(block, axis, [(i, i ^ distance) for i in devices])


def halving_sum(rows, extra, axis):
    count = lax.axis_size(axis)
    me = lax.axis_index(axis)
    bits = count.bit_length() - 1
    order = [int(format(i, "0%db" % bits)[::-1], 2) if bits else 0 for i in range(count)]
    chunks = rows.reshape(count, rows.shape[0] // count, *rows.shape[1:])
    rows = jnp.concatenate([chunks[k] for k in order], axis=0)
    distance = 1
    while distance < count:
        half = rows.shape[0] // 2
        upper = (me // distance) % 2
        keep = lax.dynamic_slice_in_dim(rows, upper * half, half, 0)
        send = lax.dynamic_slice_in_dim(rows, (1 - upper) * half, half, 0)
        got = exchanged(jnp.concatenate([send, extra], axis=0), axis, distance)
        rows = keep + got[:half]
        extra = extra + got[half:]
        distance *= 2
    return rows, extra


def doubling_sum(rows, axis):
    count = lax.axis_size(axis)
    distance = 1
    while distance < count:
        rows = rows + exchanged(rows, axis, distance)
        distance *= 2
    return rows


def doubling_gather(block, axis):
    count = lax.axis_size(axis)
    me = lax.axis_index(axis)
    distance = 1
    while distance < count:
        other = exchanged(block, axis, distance)
        mine_first = (me // distance) % 2 == 0
        block = jnp.where(
            mine_first,
            jnp.concatenate([block, other], axis=1),
            jnp.concatenate([other, block], axis=1),
        )
        distance *= 2
    return block


def spline(phase):
    rest = 1.0 - phase
    cube = phase * phase * phase
    square = phase * phase
    first = rest * rest * rest / 6.0
    second = (3.0 * cube - 6.0 * square + 4.0) / 6.0
    third = (-3.0 * cube + 3.0 * square + 3.0 * phase + 1.0) / 6.0
    fourth = cube / 6.0
    return (first, second, third, fourth)


def local(
    src_design,
    att_design,
    obs_phase,
    cal_design,
    obs_weight,
    knot_index,
    cal_block,
    cal_column,
    obs_count,
    src_res,
    att_res,
    cal_res,
    src_dir,
    att_dir,
    cal_dir,
):
    knot_count = att_dir.shape[1]
    blocks, col_width = cal_dir.shape
    all_blocks = blocks * lax.axis_size("cal")
    cal_size = all_blocks * col_width
    lane = 128
    rows = cal_size // lane
    src_rows, slots = obs_phase.shape

    cal_values = doubling_gather(cal_dir[None], "cal")[0]
    first_row = (lax.axis_index("tm") == 0).astype(jnp.float32)
    edge_knots = passed_along(att_dir[:, :3], ("tm", "cal"), -1)
    att_ext = jnp.concatenate([att_dir, edge_knots], axis=1)

    live_mask = (lax.broadcasted_iota(jnp.int32, obs_phase.shape, 1) < obs_count[:, None]).astype(
        jnp.float32
    )
    basis = spline(obs_phase)
    local_knot = knot_index - lax.axis_index(("tm", "cal")) * knot_count

    n_obs = src_rows * slots
    flat = lambda a: a.reshape(1, n_obs)

    knot_hot = (flat(local_knot) == lax.broadcasted_iota(jnp.int32, (knot_count, 1), 0)).astype(jnp.float32)

    table = jnp.stack([att_ext[:, m : m + knot_count] for m in range(4)], axis=0).reshape(12, knot_count)
    picked = jnp.dot(table, knot_hot, precision=ONE_HOT_PRECISION).reshape(4, 3, src_rows, slots)
    y_att = jnp.zeros_like(obs_phase)
    for m in range(4):
        y_att = y_att + basis[m] * jnp.sum(att_design * picked[m], axis=0)

    flat_index = flat(cal_block * col_width + cal_column)
    high_hot = (flat_index // lane == lax.broadcasted_iota(jnp.int32, (rows, 1), 0)).astype(jnp.float32)
    low_hot = (flat_index % lane == lax.broadcasted_iota(jnp.int32, (lane, 1), 0)).astype(jnp.float32)
    cal_table = cal_values.reshape(rows, lane)
    row_vals = lax.dot_general(cal_table, high_hot, (((0,), (0,)), ((), ())), precision=ONE_HOT_PRECISION)
    y_cal = cal_design * jnp.sum(row_vals * low_hot, axis=0).reshape(src_rows, slots)

    y_src = jnp.sum(src_design * src_dir[:, :, None], axis=0)
    response = live_mask * (y_src + y_att + y_cal)
    weighted = obs_weight * response
    curv_local = jnp.sum(weighted * response)
    q_src = jnp.sum(src_design * weighted[None], axis=2)

    scaled = att_design * weighted[None]
    spread = jnp.stack([basis[m][None] * scaled for m in range(4)], axis=0).reshape(12, n_obs)
    gathered = lax.dot_general(spread, knot_hot, (((1,), (1,)), ((), ())), precision=ONE_HOT_PRECISION)
    gathered = gathered.reshape(4, 3, knot_count)
    grad_ext = jnp.zeros((3, knot_count + 3), jnp.float32)
    for m in range(4):
        grad_ext = grad_ext + jnp.pad(gathered[m], ((0, 0), (m, 3 - m)))
    incoming = passed_along(grad_ext[:, knot_count:], ("tm", "cal"), 1)
    q_att = jnp.concatenate([grad_ext[:, :3] + incoming, grad_ext[:, 3:knot_count]], axis=1)

    cal_weighted = flat(cal_design * weighted) * low_hot
    cal_term = lax.dot_general(high_hot, cal_weighted, (((1,), (1,)), ((), ())), precision=ONE_HOT_PRECISION)
    res_sq = jnp.sum(src_res * src_res) + jnp.sum(att_res * att_res)
    cal_sq = first_row * jnp.sum(cal_res * cal_res)
    res_q = jnp.sum(src_res * q_src) + jnp.sum(att_res * q_att)
    q_sq = jnp.sum(q_src * q_src) + jnp.sum(q_att * q_att)
    scalars = jnp.stack([res_sq, curv_local, res_q, q_sq, cal_sq])
    scalars = jnp.concatenate([scalars, jnp.zeros((lane - 5,), jnp.float32)]).reshape(1, lane)
    own_rows, scalars = halving_sum(cal_term, scalars, "cal")
    summed = doubling_sum(jnp.concatenate([own_rows, scalars], axis=0), "tm")
    res_sq, curvature, res_q, q_sq, cal_sq = (summed[-1, k] for k in range(5))
    q_cal = summed[:-1].reshape(blocks, col_width)

    cal_dots = jnp.stack([jnp.sum(cal_res * q_cal), jnp.sum(q_cal * q_cal)])
    cal_dots = jnp.concatenate([cal_dots, jnp.zeros((lane - 2,), jnp.float32)]).reshape(1, lane)
    cal_dots = doubling_sum(cal_dots, "cal")
    res_q = res_q + cal_dots[0, 0]
    q_sq = q_sq + cal_dots[0, 1]

    norm_now = res_sq + cal_sq
    step_len = norm_now / curvature
    new_src_res = src_res - step_len * q_src
    new_att_res = att_res - step_len * q_att
    new_cal_res = cal_res - step_len * q_cal
    norm_next = norm_now - step_len * (2.0 * res_q - step_len * q_sq)
    ratio = norm_next / norm_now
    return (
        new_src_res,
        new_att_res,
        new_cal_res,
        new_src_res + ratio * src_dir,
        new_att_res + ratio * att_dir,
        new_cal_res + ratio * cal_dir,
    )


def solution(mesh):
    return jax.shard_map(
        local,
        mesh=mesh,
        in_specs=(
            P(None, ("tm", "cal"), None),
            P(None, ("tm", "cal"), None),
            P(("tm", "cal"), None),
            P(("tm", "cal"), None),
            P(("tm", "cal"), None),
            P(("tm", "cal"), None),
            P(("tm", "cal"), None),
            P(("tm", "cal"), None),
            P(("tm", "cal")),
            P(None, ("tm", "cal")),
            P(None, ("tm", "cal")),
            P("cal", None),
            P(None, ("tm", "cal")),
            P(None, ("tm", "cal")),
            P("cal", None),
        ),
        out_specs=(
            P(None, ("tm", "cal")),
            P(None, ("tm", "cal")),
            P("cal", None),
            P(None, ("tm", "cal")),
            P(None, ("tm", "cal")),
            P("cal", None),
        ),
        check_vma=False,
    )
```

```python
import jax
import jax.numpy as jnp
from jax import lax
from jax.sharding import PartitionSpec as P


ONE_HOT_PRECISION = lax.Precision.HIGH


def passed_along(block, axis, distance):
    devices = range(lax.axis_size(axis))
    route = [(i - distance, i) for i in devices if i - distance in devices]
    return lax.ppermute(block, axis, route)


def exchanged(block, axis, distance):
    devices = range(lax.axis_size(axis))
    return lax.ppermute(block, axis, [(i, i ^ distance) for i in devices])


def halving_sum(rows, extra, axis):
    count = lax.axis_size(axis)
    me = lax.axis_index(axis)
    bits = count.bit_length() - 1
    order = [int(format(i, "0%db" % bits)[::-1], 2) if bits else 0 for i in range(count)]
    chunks = rows.reshape(count, rows.shape[0] // count, *rows.shape[1:])
    rows = jnp.concatenate([chunks[k] for k in order], axis=0)
    distance = 1
    while distance < count:
        half = rows.shape[0] // 2
        upper = (me // distance) % 2
        keep = lax.dynamic_slice_in_dim(rows, upper * half, half, 0)
        send = lax.dynamic_slice_in_dim(rows, (1 - upper) * half, half, 0)
        got = exchanged(jnp.concatenate([send, extra], axis=0), axis, distance)
        rows = keep + got[:half]
        extra = extra + got[half:]
        distance *= 2
    return rows, extra


def doubling_sum(rows, axis):
    count = lax.axis_size(axis)
    distance = 1
    while distance < count:
        rows = rows + exchanged(rows, axis, distance)
        distance *= 2
    return rows


def doubling_gather(block, axis):
    count = lax.axis_size(axis)
    me = lax.axis_index(axis)
    bits = count.bit_length() - 1
    distance = count // 2
    while distance >= 1:
        other = exchanged(block, axis, distance)
        mine_first = (me // distance) % 2 == 0
        block = jnp.where(
            mine_first,
            jnp.concatenate([block, other], axis=1),
            jnp.concatenate([other, block], axis=1),
        )
        distance //= 2
    order = [int(format(i, "0%db" % bits)[::-1], 2) if bits else 0 for i in range(count)]
    parts = block.reshape(block.shape[0], count, block.shape[1] // count, *block.shape[2:])
    return jnp.concatenate([parts[:, k] for k in order], axis=1)


def spline(phase):
    rest = 1.0 - phase
    cube = phase * phase * phase
    square = phase * phase
    first = rest * rest * rest / 6.0
    second = (3.0 * cube - 6.0 * square + 4.0) / 6.0
    third = (-3.0 * cube + 3.0 * square + 3.0 * phase + 1.0) / 6.0
    fourth = cube / 6.0
    return (first, second, third, fourth)


def local(
    src_design,
    att_design,
    obs_phase,
    cal_design,
    obs_weight,
    knot_index,
    cal_block,
    cal_column,
    obs_count,
    src_res,
    att_res,
    cal_res,
    src_dir,
    att_dir,
    cal_dir,
):
    knot_count = att_dir.shape[1]
    blocks, col_width = cal_dir.shape
    all_blocks = blocks * lax.axis_size("cal")
    cal_size = all_blocks * col_width
    lane = 128
    rows = cal_size // lane
    src_rows, slots = obs_phase.shape

    cal_values = doubling_gather(cal_dir[None], "cal")[0]
    first_row = (lax.axis_index("tm") == 0).astype(jnp.float32)
    edge_knots = passed_along(att_dir[:, :3], ("tm", "cal"), -1)
    att_ext = jnp.concatenate([att_dir, edge_knots], axis=1)

    live_mask = (lax.broadcasted_iota(jnp.int32, obs_phase.shape, 1) < obs_count[:, None]).astype(
        jnp.float32
    )
    basis = spline(obs_phase)
    local_knot = knot_index - lax.axis_index(("tm", "cal")) * knot_count

    n_obs = src_rows * slots
    flat = lambda a: a.reshape(1, n_obs)

    knot_hot = (flat(local_knot) == lax.broadcasted_iota(jnp.int32, (knot_count, 1), 0)).astype(jnp.float32)

    table = jnp.stack([att_ext[:, m : m + knot_count] for m in range(4)], axis=0).reshape(12, knot_count)
    picked = jnp.dot(table, knot_hot, precision=ONE_HOT_PRECISION).reshape(4, 3, src_rows, slots)
    y_att = jnp.zeros_like(obs_phase)
    for m in range(4):
        y_att = y_att + basis[m] * jnp.sum(att_design * picked[m], axis=0)

    flat_index = flat(cal_block * col_width + cal_column)
    high_hot = (flat_index // lane == lax.broadcasted_iota(jnp.int32, (rows, 1), 0)).astype(jnp.float32)
    low_hot = (flat_index % lane == lax.broadcasted_iota(jnp.int32, (lane, 1), 0)).astype(jnp.float32)
    cal_table = cal_values.reshape(rows, lane)
    row_vals = lax.dot_general(cal_table, high_hot, (((0,), (0,)), ((), ())), precision=ONE_HOT_PRECISION)
    y_cal = cal_design * jnp.sum(row_vals * low_hot, axis=0).reshape(src_rows, slots)

    y_src = jnp.sum(src_design * src_dir[:, :, None], axis=0)
    response = live_mask * (y_src + y_att + y_cal)
    weighted = obs_weight * response
    curv_local = jnp.sum(weighted * response)
    q_src = jnp.sum(src_design * weighted[None], axis=2)

    scaled = att_design * weighted[None]
    spread = jnp.stack([basis[m][None] * scaled for m in range(4)], axis=0).reshape(12, n_obs)
    gathered = lax.dot_general(spread, knot_hot, (((1,), (1,)), ((), ())), precision=ONE_HOT_PRECISION)
    gathered = gathered.reshape(4, 3, knot_count)
    grad_ext = jnp.zeros((3, knot_count + 3), jnp.float32)
    for m in range(4):
        grad_ext = grad_ext + jnp.pad(gathered[m], ((0, 0), (m, 3 - m)))
    incoming = passed_along(grad_ext[:, knot_count:], ("tm", "cal"), 1)
    q_att = jnp.concatenate([grad_ext[:, :3] + incoming, grad_ext[:, 3:knot_count]], axis=1)

    cal_weighted = flat(cal_design * weighted) * low_hot
    cal_term = lax.dot_general(high_hot, cal_weighted, (((1,), (1,)), ((), ())), precision=ONE_HOT_PRECISION)
    res_sq = jnp.sum(src_res * src_res) + jnp.sum(att_res * att_res)
    cal_sq = first_row * jnp.sum(cal_res * cal_res)
    res_q = jnp.sum(src_res * q_src) + jnp.sum(att_res * q_att)
    q_sq = jnp.sum(q_src * q_src) + jnp.sum(q_att * q_att)
    scalars = jnp.stack([res_sq, curv_local, res_q, q_sq, cal_sq])
    scalars = jnp.concatenate([scalars, jnp.zeros((lane - 5,), jnp.float32)]).reshape(1, lane)
    own_rows, scalars = halving_sum(cal_term, scalars, "cal")
    summed = doubling_sum(jnp.concatenate([own_rows, scalars], axis=0), "tm")
    res_sq, curvature, res_q, q_sq, cal_sq = (summed[-1, k] for k in range(5))
    q_cal = summed[:-1].reshape(blocks, col_width)

    norm_now = res_sq + cal_sq
    step_len = norm_now / curvature
    new_src_res = src_res - step_len * q_src
    new_att_res = att_res - step_len * q_att
    new_cal_res = cal_res - step_len * q_cal
    kept = res_sq - step_len * (2.0 * res_q - step_len * q_sq)
    cal_next = jnp.broadcast_to(jnp.sum(new_cal_res * new_cal_res), (1, lane))
    norm_next = kept + doubling_sum(cal_next, "cal")[0, 0]
    ratio = norm_next / norm_now
    return (
        new_src_res,
        new_att_res,
        new_cal_res,
        new_src_res + ratio * src_dir,
        new_att_res + ratio * att_dir,
        new_cal_res + ratio * cal_dir,
    )


def solution(mesh):
    return jax.shard_map(
        local,
        mesh=mesh,
        in_specs=(
            P(None, ("tm", "cal"), None),
            P(None, ("tm", "cal"), None),
            P(("tm", "cal"), None),
            P(("tm", "cal"), None),
            P(("tm", "cal"), None),
            P(("tm", "cal"), None),
            P(("tm", "cal"), None),
            P(("tm", "cal"), None),
            P(("tm", "cal")),
            P(None, ("tm", "cal")),
            P(None, ("tm", "cal")),
            P("cal", None),
            P(None, ("tm", "cal")),
            P(None, ("tm", "cal")),
            P("cal", None),
        ),
        out_specs=(
            P(None, ("tm", "cal")),
            P(None, ("tm", "cal")),
            P("cal", None),
            P(None, ("tm", "cal")),
            P(None, ("tm", "cal")),
            P("cal", None),
        ),
        check_vma=False,
    )
```

```python
import jax
import jax.numpy as jnp
from jax import lax
from jax.sharding import PartitionSpec as P


ONE_HOT_PRECISION = lax.Precision.HIGH


def passed_along(block, axis, distance):
    devices = range(lax.axis_size(axis))
    route = [(i - distance, i) for i in devices if i - distance in devices]
    return lax.ppermute(block, axis, route)


def exchanged(block, axis, distance):
    devices = range(lax.axis_size(axis))
    return lax.ppermute(block, axis, [(i, i ^ distance) for i in devices])


def halving_sum(rows, extra, axis):
    count = lax.axis_size(axis)
    me = lax.axis_index(axis)
    bits = count.bit_length() - 1
    order = [int(format(i, "0%db" % bits)[::-1], 2) if bits else 0 for i in range(count)]
    chunks = rows.reshape(count, rows.shape[0] // count, *rows.shape[1:])
    rows = jnp.concatenate([chunks[k] for k in order], axis=0)
    distance = 1
    while distance < count:
        half = rows.shape[0] // 2
        upper = (me // distance) % 2
        keep = lax.dynamic_slice_in_dim(rows, upper * half, half, 0)
        send = lax.dynamic_slice_in_dim(rows, (1 - upper) * half, half, 0)
        got = exchanged(jnp.concatenate([send, extra], axis=0), axis, distance)
        rows = keep + got[:half]
        extra = extra + got[half:]
        distance *= 2
    return rows, extra


def doubling_sum(rows, axis):
    count = lax.axis_size(axis)
    distance = count // 2
    while distance >= 1:
        rows = rows + exchanged(rows, axis, distance)
        distance //= 2
    return rows


def doubling_gather(block, axis):
    count = lax.axis_size(axis)
    me = lax.axis_index(axis)
    bits = count.bit_length() - 1
    distance = count // 2
    while distance >= 1:
        other = exchanged(block, axis, distance)
        mine_first = (me // distance) % 2 == 0
        block = jnp.where(
            mine_first,
            jnp.concatenate([block, other], axis=1),
            jnp.concatenate([other, block], axis=1),
        )
        distance //= 2
    order = [int(format(i, "0%db" % bits)[::-1], 2) if bits else 0 for i in range(count)]
    parts = block.reshape(block.shape[0], count, block.shape[1] // count, *block.shape[2:])
    return jnp.concatenate([parts[:, k] for k in order], axis=1)


def spline(phase):
    rest = 1.0 - phase
    cube = phase * phase * phase
    square = phase * phase
    first = rest * rest * rest / 6.0
    second = (3.0 * cube - 6.0 * square + 4.0) / 6.0
    third = (-3.0 * cube + 3.0 * square + 3.0 * phase + 1.0) / 6.0
    fourth = cube / 6.0
    return (first, second, third, fourth)


def local(
    src_design,
    att_design,
    obs_phase,
    cal_design,
    obs_weight,
    knot_index,
    cal_block,
    cal_column,
    obs_count,
    src_res,
    att_res,
    cal_res,
    src_dir,
    att_dir,
    cal_dir,
):
    knot_count = att_dir.shape[1]
    blocks, col_width = cal_dir.shape
    all_blocks = blocks * lax.axis_size("cal")
    cal_size = all_blocks * col_width
    lane = 128
    rows = cal_size // lane
    src_rows, slots = obs_phase.shape

    cal_values = doubling_gather(cal_dir[None], "cal")[0]
    first_row = (lax.axis_index("tm") == 0).astype(jnp.float32)
    edge_knots = passed_along(att_dir[:, :3], ("tm", "cal"), -1)
    att_ext = jnp.concatenate([att_dir, edge_knots], axis=1)

    live_mask = (lax.broadcasted_iota(jnp.int32, obs_phase.shape, 1) < obs_count[:, None]).astype(
        jnp.float32
    )
    basis = spline(obs_phase)
    local_knot = knot_index - lax.axis_index(("tm", "cal")) * knot_count

    n_obs = src_rows * slots
    flat = lambda a: a.reshape(1, n_obs)

    knot_hot = (flat(local_knot) == lax.broadcasted_iota(jnp.int32, (knot_count, 1), 0)).astype(jnp.float32)

    table = jnp.stack([att_ext[:, m : m + knot_count] for m in range(4)], axis=0).reshape(12, knot_count)
    picked = jnp.dot(table, knot_hot, precision=ONE_HOT_PRECISION).reshape(4, 3, src_rows, slots)
    y_att = jnp.zeros_like(obs_phase)
    for m in range(4):
        y_att = y_att + basis[m] * jnp.sum(att_design * picked[m], axis=0)

    flat_index = flat(cal_block * col_width + cal_column)
    high_hot = (flat_index // lane == lax.broadcasted_iota(jnp.int32, (rows, 1), 0)).astype(jnp.float32)
    low_hot = (flat_index % lane == lax.broadcasted_iota(jnp.int32, (lane, 1), 0)).astype(jnp.float32)
    cal_table = cal_values.reshape(rows, lane)
    row_vals = lax.dot_general(cal_table, high_hot, (((0,), (0,)), ((), ())), precision=ONE_HOT_PRECISION)
    y_cal = cal_design * jnp.sum(row_vals * low_hot, axis=0).reshape(src_rows, slots)

    y_src = jnp.sum(src_design * src_dir[:, :, None], axis=0)
    response = live_mask * (y_src + y_att + y_cal)
    weighted = obs_weight * response
    curv_local = jnp.sum(weighted * response)
    q_src = jnp.sum(src_design * weighted[None], axis=2)

    scaled = att_design * weighted[None]
    spread = jnp.stack([basis[m][None] * scaled for m in range(4)], axis=0).reshape(12, n_obs)
    gathered = lax.dot_general(spread, knot_hot, (((1,), (1,)), ((), ())), precision=ONE_HOT_PRECISION)
    gathered = gathered.reshape(4, 3, knot_count)
    grad_ext = jnp.zeros((3, knot_count + 3), jnp.float32)
    for m in range(4):
        grad_ext = grad_ext + jnp.pad(gathered[m], ((0, 0), (m, 3 - m)))
    incoming = passed_along(grad_ext[:, knot_count:], ("tm", "cal"), 1)
    q_att = jnp.concatenate([grad_ext[:, :3] + incoming, grad_ext[:, 3:knot_count]], axis=1)

    cal_weighted = flat(cal_design * weighted) * low_hot
    cal_term = lax.dot_general(high_hot, cal_weighted, (((1,), (1,)), ((), ())), precision=ONE_HOT_PRECISION)
    res_sq = jnp.sum(src_res * src_res) + jnp.sum(att_res * att_res)
    cal_sq = first_row * jnp.sum(cal_res * cal_res)
    res_q = jnp.sum(src_res * q_src) + jnp.sum(att_res * q_att)
    q_sq = jnp.sum(q_src * q_src) + jnp.sum(q_att * q_att)
    scalars = jnp.stack([res_sq, curv_local, res_q, q_sq, cal_sq])
    scalars = jnp.concatenate([scalars, jnp.zeros((lane - 5,), jnp.float32)]).reshape(1, lane)
    own_rows, scalars = halving_sum(cal_term, scalars, "cal")
    summed = doubling_sum(jnp.concatenate([own_rows, scalars], axis=0), "tm")
    res_sq, curvature, res_q, q_sq, cal_sq = (summed[-1, k] for k in range(5))
    q_cal = summed[:-1].reshape(blocks, col_width)

    norm_now = res_sq + cal_sq
    step_len = norm_now / curvature
    new_src_res = src_res - step_len * q_src
    new_att_res = att_res - step_len * q_att
    new_cal_res = cal_res - step_len * q_cal
    kept = res_sq - step_len * (2.0 * res_q - step_len * q_sq)
    cal_next = jnp.broadcast_to(jnp.sum(new_cal_res * new_cal_res), (1, lane))
    norm_next = kept + doubling_sum(cal_next, "cal")[0, 0]
    ratio = norm_next / norm_now
    return (
        new_src_res,
        new_att_res,
        new_cal_res,
        new_src_res + ratio * src_dir,
        new_att_res + ratio * att_dir,
        new_cal_res + ratio * cal_dir,
    )


def solution(mesh):
    return jax.shard_map(
        local,
        mesh=mesh,
        in_specs=(
            P(None, ("tm", "cal"), None),
            P(None, ("tm", "cal"), None),
            P(("tm", "cal"), None),
            P(("tm", "cal"), None),
            P(("tm", "cal"), None),
            P(("tm", "cal"), None),
            P(("tm", "cal"), None),
            P(("tm", "cal"), None),
            P(("tm", "cal")),
            P(None, ("tm", "cal")),
            P(None, ("tm", "cal")),
            P("cal", None),
            P(None, ("tm", "cal")),
            P(None, ("tm", "cal")),
            P("cal", None),
        ),
        out_specs=(
            P(None, ("tm", "cal")),
            P(None, ("tm", "cal")),
            P("cal", None),
            P(None, ("tm", "cal")),
            P(None, ("tm", "cal")),
            P("cal", None),
        ),
        check_vma=False,
    )
```

```python
import jax
import jax.numpy as jnp
from jax import lax
from jax.sharding import PartitionSpec as P


ONE_HOT_PRECISION = lax.Precision.HIGH


def passed_along(block, axis, distance):
    devices = range(lax.axis_size(axis))
    route = [(i - distance, i) for i in devices if i - distance in devices]
    return lax.ppermute(block, axis, route)


def exchanged(block, axis, distance):
    devices = range(lax.axis_size(axis))
    return lax.ppermute(block, axis, [(i, i ^ distance) for i in devices])


def halving_sum(rows, extra, axis):
    count = lax.axis_size(axis)
    me = lax.axis_index(axis)
    bits = count.bit_length() - 1
    order = [int(format(i, "0%db" % bits)[::-1], 2) if bits else 0 for i in range(count)]
    chunks = rows.reshape(count, rows.shape[0] // count, *rows.shape[1:])
    rows = jnp.concatenate([chunks[k] for k in order], axis=0)
    distance = 1
    while distance < count:
        half = rows.shape[0] // 2
        upper = (me // distance) % 2
        keep = lax.dynamic_slice_in_dim(rows, upper * half, half, 0)
        send = lax.dynamic_slice_in_dim(rows, (1 - upper) * half, half, 0)
        got = exchanged(jnp.concatenate([send, extra], axis=0), axis, distance)
        rows = keep + got[:half]
        extra = extra + got[half:]
        distance *= 2
    return rows, extra


def doubling_sum(rows, axis):
    count = lax.axis_size(axis)
    distance = 1
    while distance < count:
        rows = rows + exchanged(rows, axis, distance)
        distance *= 2
    return rows


def doubling_gather(block, axis):
    count = lax.axis_size(axis)
    me = lax.axis_index(axis)
    bits = count.bit_length() - 1
    distance = count // 2
    while distance >= 1:
        other = exchanged(block, axis, distance)
        mine_first = (me // distance) % 2 == 0
        block = jnp.where(
            mine_first,
            jnp.concatenate([block, other], axis=1),
            jnp.concatenate([other, block], axis=1),
        )
        distance //= 2
    order = [int(format(i, "0%db" % bits)[::-1], 2) if bits else 0 for i in range(count)]
    parts = block.reshape(block.shape[0], count, block.shape[1] // count, *block.shape[2:])
    return jnp.concatenate([parts[:, k] for k in order], axis=1)


def spline(phase):
    rest = 1.0 - phase
    cube = phase * phase * phase
    square = phase * phase
    first = rest * rest * rest / 6.0
    second = (3.0 * cube - 6.0 * square + 4.0) / 6.0
    third = (-3.0 * cube + 3.0 * square + 3.0 * phase + 1.0) / 6.0
    fourth = cube / 6.0
    return (first, second, third, fourth)


def local(
    src_design,
    att_design,
    obs_phase,
    cal_design,
    obs_weight,
    knot_index,
    cal_block,
    cal_column,
    obs_count,
    src_res,
    att_res,
    cal_res,
    src_dir,
    att_dir,
    cal_dir,
):
    knot_count = att_dir.shape[1]
    blocks, col_width = cal_dir.shape
    all_blocks = blocks * lax.axis_size("cal")
    cal_size = all_blocks * col_width
    lane = 128
    rows = cal_size // lane
    src_rows, slots = obs_phase.shape

    cal_values = doubling_gather(cal_dir[None], "cal")[0]
    first_row = (lax.axis_index("tm") == 0).astype(jnp.float32)
    edge_knots = passed_along(att_dir[:, :3], ("tm", "cal"), -1)
    att_ext = jnp.concatenate([att_dir, edge_knots], axis=1)

    live_mask = (lax.broadcasted_iota(jnp.int32, obs_phase.shape, 1) < obs_count[:, None]).astype(
        jnp.float32
    )
    basis = spline(obs_phase)
    local_knot = knot_index - lax.axis_index(("tm", "cal")) * knot_count

    n_obs = src_rows * slots
    flat = lambda a: a.reshape(1, n_obs)

    knot_hot = (flat(local_knot) == lax.broadcasted_iota(jnp.int32, (knot_count, 1), 0)).astype(jnp.float32)

    table = jnp.stack([att_ext[:, m : m + knot_count] for m in range(4)], axis=0).reshape(12, knot_count)
    picked = jnp.dot(table, knot_hot, precision=ONE_HOT_PRECISION).reshape(4, 3, src_rows, slots)
    y_att = jnp.zeros_like(obs_phase)
    for m in range(4):
        y_att = y_att + basis[m] * jnp.sum(att_design * picked[m], axis=0)

    flat_index = flat(cal_block * col_width + cal_column)
    high_hot = (flat_index // lane == lax.broadcasted_iota(jnp.int32, (rows, 1), 0)).astype(jnp.float32)
    low_hot = (flat_index % lane == lax.broadcasted_iota(jnp.int32, (lane, 1), 0)).astype(jnp.float32)
    cal_table = cal_values.reshape(rows, lane)
    row_vals = lax.dot_general(cal_table, high_hot, (((0,), (0,)), ((), ())), precision=ONE_HOT_PRECISION)
    y_cal = cal_design * jnp.sum(row_vals * low_hot, axis=0).reshape(src_rows, slots)

    y_src = jnp.sum(src_design * src_dir[:, :, None], axis=0)
    response = live_mask * (y_src + y_att + y_cal)
    weighted = obs_weight * response
    curv_local = jnp.sum(weighted * response)
    q_src = jnp.sum(src_design * weighted[None], axis=2)

    scaled = att_design * weighted[None]
    spread = jnp.stack([basis[m][None] * scaled for m in range(4)], axis=0).reshape(12, n_obs)
    gathered = lax.dot_general(spread, knot_hot, (((1,), (1,)), ((), ())), precision=ONE_HOT_PRECISION)
    gathered = gathered.reshape(4, 3, knot_count)
    grad_ext = jnp.zeros((3, knot_count + 3), jnp.float32)
    for m in range(4):
        grad_ext = grad_ext + jnp.pad(gathered[m], ((0, 0), (m, 3 - m)))
    incoming = passed_along(grad_ext[:, knot_count:], ("tm", "cal"), 1)
    q_att = jnp.concatenate([grad_ext[:, :3] + incoming, grad_ext[:, 3:knot_count]], axis=1)

    cal_weighted = flat(cal_design * weighted) * low_hot
    cal_term = lax.dot_general(high_hot, cal_weighted, (((1,), (1,)), ((), ())), precision=ONE_HOT_PRECISION)
    res_sq = jnp.sum(src_res * src_res) + jnp.sum(att_res * att_res)
    cal_sq = first_row * jnp.sum(cal_res * cal_res)
    res_q = jnp.sum(src_res * q_src) + jnp.sum(att_res * q_att)
    q_sq = jnp.sum(q_src * q_src) + jnp.sum(q_att * q_att)
    scalars = jnp.stack([res_sq, curv_local, res_q, q_sq, cal_sq])
    scalars = jnp.concatenate([scalars, jnp.zeros((lane - 5,), jnp.float32)]).reshape(1, lane)
    own_rows, scalars = halving_sum(cal_term, scalars, "cal")
    summed = doubling_sum(jnp.concatenate([own_rows, scalars], axis=0), "tm")
    res_sq, curvature, res_q, q_sq, cal_sq = (summed[-1, k] for k in range(5))
    q_cal = summed[:-1].reshape(blocks, col_width)

    norm_now = res_sq + cal_sq
    step_len = norm_now / curvature
    new_src_res = src_res - step_len * q_src
    new_att_res = att_res - step_len * q_att
    new_cal_res = cal_res - step_len * q_cal
    kept = res_sq - step_len * (2.0 * res_q - step_len * q_sq)
    cal_next = jnp.broadcast_to(jnp.sum(new_cal_res * new_cal_res), (1, lane))
    cal_next = cal_next + exchanged(cal_next, "cal", 2)
    norm_next = kept + (cal_next + exchanged(cal_next, "cal", 1))[0, 0]
    ratio = norm_next / norm_now
    return (
        new_src_res,
        new_att_res,
        new_cal_res,
        new_src_res + ratio * src_dir,
        new_att_res + ratio * att_dir,
        new_cal_res + ratio * cal_dir,
    )


def solution(mesh):
    return jax.shard_map(
        local,
        mesh=mesh,
        in_specs=(
            P(None, ("tm", "cal"), None),
            P(None, ("tm", "cal"), None),
            P(("tm", "cal"), None),
            P(("tm", "cal"), None),
            P(("tm", "cal"), None),
            P(("tm", "cal"), None),
            P(("tm", "cal"), None),
            P(("tm", "cal"), None),
            P(("tm", "cal")),
            P(None, ("tm", "cal")),
            P(None, ("tm", "cal")),
            P("cal", None),
            P(None, ("tm", "cal")),
            P(None, ("tm", "cal")),
            P("cal", None),
        ),
        out_specs=(
            P(None, ("tm", "cal")),
            P(None, ("tm", "cal")),
            P("cal", None),
            P(None, ("tm", "cal")),
            P(None, ("tm", "cal")),
            P("cal", None),
        ),
        check_vma=False,
    )
```

```python
import jax
import jax.numpy as jnp
from jax import lax
from jax.sharding import PartitionSpec as P


ONE_HOT_PRECISION = lax.Precision.HIGH


def passed_along(block, axis, distance):
    devices = range(lax.axis_size(axis))
    route = [(i - distance, i) for i in devices if i - distance in devices]
    return lax.ppermute(block, axis, route)


def exchanged(block, axis, distance):
    devices = range(lax.axis_size(axis))
    return lax.ppermute(block, axis, [(i, i ^ distance) for i in devices])


def halving_sum(rows, extra, axis):
    count = lax.axis_size(axis)
    me = lax.axis_index(axis)
    bits = count.bit_length() - 1
    order = [int(format(i, "0%db" % bits)[::-1], 2) if bits else 0 for i in range(count)]
    chunks = rows.reshape(count, rows.shape[0] // count, *rows.shape[1:])
    rows = jnp.concatenate([chunks[k] for k in order], axis=0)
    distance = 1
    while distance < count:
        half = rows.shape[0] // 2
        upper = (me // distance) % 2
        keep = lax.dynamic_slice_in_dim(rows, upper * half, half, 0)
        send = lax.dynamic_slice_in_dim(rows, (1 - upper) * half, half, 0)
        if distance == 1:
            rows = keep + exchanged(send, axis, distance)
            extra = extra + exchanged(extra, axis, distance)
        else:
            got = exchanged(jnp.concatenate([send, extra], axis=0), axis, distance)
            rows = keep + got[:half]
            extra = extra + got[half:]
        distance *= 2
    return rows, extra


def doubling_sum(rows, axis):
    count = lax.axis_size(axis)
    distance = 1
    while distance < count:
        rows = rows + exchanged(rows, axis, distance)
        distance *= 2
    return rows


def doubling_gather(block, axis):
    count = lax.axis_size(axis)
    me = lax.axis_index(axis)
    bits = count.bit_length() - 1
    distance = count // 2
    while distance >= 1:
        other = exchanged(block, axis, distance)
        mine_first = (me // distance) % 2 == 0
        block = jnp.where(
            mine_first,
            jnp.concatenate([block, other], axis=1),
            jnp.concatenate([other, block], axis=1),
        )
        distance //= 2
    order = [int(format(i, "0%db" % bits)[::-1], 2) if bits else 0 for i in range(count)]
    parts = block.reshape(block.shape[0], count, block.shape[1] // count, *block.shape[2:])
    return jnp.concatenate([parts[:, k] for k in order], axis=1)


def spline(phase):
    rest = 1.0 - phase
    cube = phase * phase * phase
    square = phase * phase
    first = rest * rest * rest / 6.0
    second = (3.0 * cube - 6.0 * square + 4.0) / 6.0
    third = (-3.0 * cube + 3.0 * square + 3.0 * phase + 1.0) / 6.0
    fourth = cube / 6.0
    return (first, second, third, fourth)


def local(
    src_design,
    att_design,
    obs_phase,
    cal_design,
    obs_weight,
    knot_index,
    cal_block,
    cal_column,
    obs_count,
    src_res,
    att_res,
    cal_res,
    src_dir,
    att_dir,
    cal_dir,
):
    knot_count = att_dir.shape[1]
    blocks, col_width = cal_dir.shape
    all_blocks = blocks * lax.axis_size("cal")
    cal_size = all_blocks * col_width
    lane = 128
    rows = cal_size // lane
    src_rows, slots = obs_phase.shape

    cal_values = doubling_gather(cal_dir[None], "cal")[0]
    first_row = (lax.axis_index("tm") == 0).astype(jnp.float32)
    edge_knots = passed_along(att_dir[:, :3], ("tm", "cal"), -1)
    att_ext = jnp.concatenate([att_dir, edge_knots], axis=1)

    live_mask = (lax.broadcasted_iota(jnp.int32, obs_phase.shape, 1) < obs_count[:, None]).astype(
        jnp.float32
    )
    basis = spline(obs_phase)
    local_knot = knot_index - lax.axis_index(("tm", "cal")) * knot_count

    n_obs = src_rows * slots
    flat = lambda a: a.reshape(1, n_obs)

    knot_hot = (flat(local_knot) == lax.broadcasted_iota(jnp.int32, (knot_count, 1), 0)).astype(jnp.float32)

    table = jnp.stack([att_ext[:, m : m + knot_count] for m in range(4)], axis=0).reshape(12, knot_count)
    picked = jnp.dot(table, knot_hot, precision=ONE_HOT_PRECISION).reshape(4, 3, src_rows, slots)
    y_att = jnp.zeros_like(obs_phase)
    for m in range(4):
        y_att = y_att + basis[m] * jnp.sum(att_design * picked[m], axis=0)

    flat_index = flat(cal_block * col_width + cal_column)
    high_hot = (flat_index // lane == lax.broadcasted_iota(jnp.int32, (rows, 1), 0)).astype(jnp.float32)
    low_hot = (flat_index % lane == lax.broadcasted_iota(jnp.int32, (lane, 1), 0)).astype(jnp.float32)
    cal_table = cal_values.reshape(rows, lane)
    row_vals = lax.dot_general(cal_table, high_hot, (((0,), (0,)), ((), ())), precision=ONE_HOT_PRECISION)
    y_cal = cal_design * jnp.sum(row_vals * low_hot, axis=0).reshape(src_rows, slots)

    y_src = jnp.sum(src_design * src_dir[:, :, None], axis=0)
    response = live_mask * (y_src + y_att + y_cal)
    weighted = obs_weight * response
    curv_local = jnp.sum(weighted * response)
    q_src = jnp.sum(src_design * weighted[None], axis=2)

    scaled = att_design * weighted[None]
    spread = jnp.stack([basis[m][None] * scaled for m in range(4)], axis=0).reshape(12, n_obs)
    gathered = lax.dot_general(spread, knot_hot, (((1,), (1,)), ((), ())), precision=ONE_HOT_PRECISION)
    gathered = gathered.reshape(4, 3, knot_count)
    grad_ext = jnp.zeros((3, knot_count + 3), jnp.float32)
    for m in range(4):
        grad_ext = grad_ext + jnp.pad(gathered[m], ((0, 0), (m, 3 - m)))
    incoming = passed_along(grad_ext[:, knot_count:], ("tm", "cal"), 1)
    q_att = jnp.concatenate([grad_ext[:, :3] + incoming, grad_ext[:, 3:knot_count]], axis=1)

    cal_weighted = flat(cal_design * weighted) * low_hot
    cal_term = lax.dot_general(high_hot, cal_weighted, (((1,), (1,)), ((), ())), precision=ONE_HOT_PRECISION)
    res_sq = jnp.sum(src_res * src_res) + jnp.sum(att_res * att_res)
    cal_sq = first_row * jnp.sum(cal_res * cal_res)
    res_q = jnp.sum(src_res * q_src) + jnp.sum(att_res * q_att)
    q_sq = jnp.sum(q_src * q_src) + jnp.sum(q_att * q_att)
    scalars = jnp.stack([res_sq, curv_local, res_q, q_sq, cal_sq])
    scalars = jnp.concatenate([scalars, jnp.zeros((lane - 5,), jnp.float32)]).reshape(1, lane)
    own_rows, scalars = halving_sum(cal_term, scalars, "cal")
    summed = doubling_sum(jnp.concatenate([own_rows, scalars], axis=0), "tm")
    res_sq, curvature, res_q, q_sq, cal_sq = (summed[-1, k] for k in range(5))
    q_cal = summed[:-1].reshape(blocks, col_width)

    norm_now = res_sq + cal_sq
    step_len = norm_now / curvature
    new_src_res = src_res - step_len * q_src
    new_att_res = att_res - step_len * q_att
    new_cal_res = cal_res - step_len * q_cal
    kept = res_sq - step_len * (2.0 * res_q - step_len * q_sq)
    cal_next = jnp.broadcast_to(jnp.sum(new_cal_res * new_cal_res), (1, lane))
    norm_next = kept + doubling_sum(cal_next, "cal")[0, 0]
    ratio = norm_next / norm_now
    return (
        new_src_res,
        new_att_res,
        new_cal_res,
        new_src_res + ratio * src_dir,
        new_att_res + ratio * att_dir,
        new_cal_res + ratio * cal_dir,
    )


def solution(mesh):
    return jax.shard_map(
        local,
        mesh=mesh,
        in_specs=(
            P(None, ("tm", "cal"), None),
            P(None, ("tm", "cal"), None),
            P(("tm", "cal"), None),
            P(("tm", "cal"), None),
            P(("tm", "cal"), None),
            P(("tm", "cal"), None),
            P(("tm", "cal"), None),
            P(("tm", "cal"), None),
            P(("tm", "cal")),
            P(None, ("tm", "cal")),
            P(None, ("tm", "cal")),
            P("cal", None),
            P(None, ("tm", "cal")),
            P(None, ("tm", "cal")),
            P("cal", None),
        ),
        out_specs=(
            P(None, ("tm", "cal")),
            P(None, ("tm", "cal")),
            P("cal", None),
            P(None, ("tm", "cal")),
            P(None, ("tm", "cal")),
            P("cal", None),
        ),
        check_vma=False,
    )
```

```python
import jax
import jax.numpy as jnp
from jax import lax
from jax.sharding import PartitionSpec as P


ONE_HOT_PRECISION = lax.Precision.HIGH


def passed_along(block, axis, distance):
    devices = range(lax.axis_size(axis))
    route = [(i - distance, i) for i in devices if i - distance in devices]
    return lax.ppermute(block, axis, route)


def exchanged(block, axis, distance):
    devices = range(lax.axis_size(axis))
    return lax.ppermute(block, axis, [(i, i ^ distance) for i in devices])


def halving_sum(rows, extra, axis):
    count = lax.axis_size(axis)
    me = lax.axis_index(axis)
    bits = count.bit_length() - 1
    order = [int(format(i, "0%db" % bits)[::-1], 2) if bits else 0 for i in range(count)]
    chunks = rows.reshape(count, rows.shape[0] // count, *rows.shape[1:])
    rows = jnp.concatenate([chunks[k] for k in order], axis=0)
    distance = 1
    while distance < count:
        half = rows.shape[0] // 2
        upper = (me // distance) % 2
        keep = lax.dynamic_slice_in_dim(rows, upper * half, half, 0)
        send = lax.dynamic_slice_in_dim(rows, (1 - upper) * half, half, 0)
        got = exchanged(jnp.concatenate([send, extra], axis=0), axis, distance)
        rows = keep + got[:half]
        extra = extra + got[half:]
        distance *= 2
    return rows, extra


def doubling_sum(rows, axis):
    count = lax.axis_size(axis)
    distance = 1
    while distance < count:
        rows = rows + exchanged(rows, axis, distance)
        distance *= 2
    return rows


def doubling_gather(block, axis):
    count = lax.axis_size(axis)
    me = lax.axis_index(axis)
    bits = count.bit_length() - 1
    distance = count // 2
    while distance >= 1:
        other = exchanged(block, axis, distance)
        mine_first = (me // distance) % 2 == 0
        block = jnp.where(
            mine_first,
            jnp.concatenate([block, other], axis=1),
            jnp.concatenate([other, block], axis=1),
        )
        distance //= 2
    order = [int(format(i, "0%db" % bits)[::-1], 2) if bits else 0 for i in range(count)]
    parts = block.reshape(block.shape[0], count, block.shape[1] // count, *block.shape[2:])
    return jnp.concatenate([parts[:, k] for k in order], axis=1)


def spline(phase):
    rest = 1.0 - phase
    cube = phase * phase * phase
    square = phase * phase
    first = rest * rest * rest / 6.0
    second = (3.0 * cube - 6.0 * square + 4.0) / 6.0
    third = (-3.0 * cube + 3.0 * square + 3.0 * phase + 1.0) / 6.0
    fourth = cube / 6.0
    return (first, second, third, fourth)


def local(
    src_design,
    att_design,
    obs_phase,
    cal_design,
    obs_weight,
    knot_index,
    cal_block,
    cal_column,
    obs_count,
    src_res,
    att_res,
    cal_res,
    src_dir,
    att_dir,
    cal_dir,
):
    knot_count = att_dir.shape[1]
    blocks, col_width = cal_dir.shape
    all_blocks = blocks * lax.axis_size("cal")
    cal_size = all_blocks * col_width
    lane = 128
    rows = cal_size // lane
    src_rows, slots = obs_phase.shape

    cal_values = doubling_gather(cal_dir[None], "cal")[0]
    first_row = (lax.axis_index("tm") == 0).astype(jnp.float32)
    edge_knots = passed_along(att_dir[:, :3], ("tm", "cal"), -1)
    att_ext = jnp.concatenate([att_dir, edge_knots], axis=1)

    live_mask = (lax.broadcasted_iota(jnp.int32, obs_phase.shape, 1) < obs_count[:, None]).astype(
        jnp.float32
    )
    basis = spline(obs_phase)
    local_knot = knot_index - lax.axis_index(("tm", "cal")) * knot_count

    n_obs = src_rows * slots
    flat = lambda a: a.reshape(1, n_obs)

    knot_hot = (flat(local_knot) == lax.broadcasted_iota(jnp.int32, (knot_count, 1), 0)).astype(jnp.float32)

    table = jnp.stack([att_ext[:, m : m + knot_count] for m in range(4)], axis=0).reshape(12, knot_count)
    picked = jnp.dot(table, knot_hot, precision=ONE_HOT_PRECISION).reshape(4, 3, src_rows, slots)
    y_att = jnp.zeros_like(obs_phase)
    for m in range(4):
        y_att = y_att + basis[m] * jnp.sum(att_design * picked[m], axis=0)

    flat_index = flat(cal_block * col_width + cal_column)
    high_hot = (flat_index // lane == lax.broadcasted_iota(jnp.int32, (rows, 1), 0)).astype(jnp.float32)
    low_hot = (flat_index % lane == lax.broadcasted_iota(jnp.int32, (lane, 1), 0)).astype(jnp.float32)
    cal_table = cal_values.reshape(rows, lane)
    row_vals = lax.dot_general(cal_table, high_hot, (((0,), (0,)), ((), ())), precision=ONE_HOT_PRECISION)
    y_cal = cal_design * jnp.sum(row_vals * low_hot, axis=0).reshape(src_rows, slots)

    y_src = jnp.sum(src_design * src_dir[:, :, None], axis=0)
    response = live_mask * (y_src + y_att + y_cal)
    weighted = obs_weight * response
    curv_local = jnp.sum(weighted * response)
    q_src = jnp.sum(src_design * weighted[None], axis=2)

    scaled = att_design * weighted[None]
    spread = jnp.stack([basis[m][None] * scaled for m in range(4)], axis=0).reshape(12, n_obs)
    gathered = lax.dot_general(spread, knot_hot, (((1,), (1,)), ((), ())), precision=ONE_HOT_PRECISION)
    gathered = gathered.reshape(4, 3, knot_count)
    grad_ext = jnp.zeros((3, knot_count + 3), jnp.float32)
    for m in range(4):
        grad_ext = grad_ext + jnp.pad(gathered[m], ((0, 0), (m, 3 - m)))
    incoming = passed_along(grad_ext[:, knot_count:], ("tm", "cal"), 1)
    q_att = jnp.concatenate([grad_ext[:, :3] + incoming, grad_ext[:, 3:knot_count]], axis=1)

    cal_weighted = flat(cal_design * weighted) * low_hot
    cal_term = lax.dot_general(high_hot, cal_weighted, (((1,), (1,)), ((), ())), precision=ONE_HOT_PRECISION)
    res_sq = jnp.sum(src_res * src_res) + jnp.sum(att_res * att_res)
    cal_sq = first_row * jnp.sum(cal_res * cal_res)
    res_q = jnp.sum(src_res * q_src) + jnp.sum(att_res * q_att)
    q_sq = jnp.sum(q_src * q_src) + jnp.sum(q_att * q_att)
    scalars = jnp.stack([res_sq, curv_local, res_q, q_sq, cal_sq])
    scalars = jnp.concatenate([scalars, jnp.zeros((lane - 5,), jnp.float32)]).reshape(1, lane)
    own_rows, scalars = halving_sum(cal_term, scalars, "cal")
    summed = doubling_sum(jnp.concatenate([own_rows, scalars], axis=0), "tm")
    res_sq, curvature, res_q, q_sq, cal_sq = (summed[-1, k] for k in range(5))
    q_cal = summed[:-1].reshape(blocks, col_width)

    norm_now = res_sq + cal_sq
    step_len = norm_now / curvature
    new_src_res = src_res - step_len * q_src
    new_att_res = att_res - step_len * q_att
    new_cal_res = cal_res - step_len * q_cal
    kept = res_sq - step_len * (2.0 * res_q - step_len * q_sq)
    cal_next = jnp.sum(new_cal_res * new_cal_res, keepdims=True)
    norm_next = kept + doubling_sum(cal_next, "cal")[0, 0]
    ratio = norm_next / norm_now
    return (
        new_src_res,
        new_att_res,
        new_cal_res,
        new_src_res + ratio * src_dir,
        new_att_res + ratio * att_dir,
        new_cal_res + ratio * cal_dir,
    )


def solution(mesh):
    return jax.shard_map(
        local,
        mesh=mesh,
        in_specs=(
            P(None, ("tm", "cal"), None),
            P(None, ("tm", "cal"), None),
            P(("tm", "cal"), None),
            P(("tm", "cal"), None),
            P(("tm", "cal"), None),
            P(("tm", "cal"), None),
            P(("tm", "cal"), None),
            P(("tm", "cal"), None),
            P(("tm", "cal")),
            P(None, ("tm", "cal")),
            P(None, ("tm", "cal")),
            P("cal", None),
            P(None, ("tm", "cal")),
            P(None, ("tm", "cal")),
            P("cal", None),
        ),
        out_specs=(
            P(None, ("tm", "cal")),
            P(None, ("tm", "cal")),
            P("cal", None),
            P(None, ("tm", "cal")),
            P(None, ("tm", "cal")),
            P("cal", None),
        ),
        check_vma=False,
    )
```

```python
import jax
import jax.numpy as jnp
from jax import lax
from jax.sharding import PartitionSpec as P


ONE_HOT_PRECISION = lax.Precision.HIGH


def passed_along(block, axis, distance):
    devices = range(lax.axis_size(axis))
    route = [(i - distance, i) for i in devices if i - distance in devices]
    return lax.ppermute(block, axis, route)


def exchanged(block, axis, distance):
    devices = range(lax.axis_size(axis))
    return lax.ppermute(block, axis, [(i, i ^ distance) for i in devices])


def halving_sum(rows, extra, axis):
    count = lax.axis_size(axis)
    me = lax.axis_index(axis)
    bits = count.bit_length() - 1
    order = [int(format(i, "0%db" % bits)[::-1], 2) if bits else 0 for i in range(count)]
    chunks = rows.reshape(count, rows.shape[0] // count, *rows.shape[1:])
    rows = jnp.concatenate([chunks[k] for k in order], axis=0)
    distance = 1
    while distance < count:
        half = rows.shape[0] // 2
        upper = (me // distance) % 2
        keep = lax.dynamic_slice_in_dim(rows, upper * half, half, 0)
        send = lax.dynamic_slice_in_dim(rows, (1 - upper) * half, half, 0)
        got = exchanged(jnp.concatenate([send, extra], axis=0), axis, distance)
        rows = keep + got[:half]
        extra = extra + got[half:]
        distance *= 2
    return rows, extra


def doubling_sum(rows, axis):
    count = lax.axis_size(axis)
    distance = 1
    while distance < count:
        rows = rows + exchanged(rows, axis, distance)
        distance *= 2
    return rows


def doubling_gather(block, axis):
    count = lax.axis_size(axis)
    me = lax.axis_index(axis)
    bits = count.bit_length() - 1
    distance = count // 2
    while distance >= 1:
        other = exchanged(block, axis, distance)
        mine_first = (me // distance) % 2 == 0
        block = jnp.where(
            mine_first,
            jnp.concatenate([block, other], axis=1),
            jnp.concatenate([other, block], axis=1),
        )
        distance //= 2
    order = [int(format(i, "0%db" % bits)[::-1], 2) if bits else 0 for i in range(count)]
    parts = block.reshape(block.shape[0], count, block.shape[1] // count, *block.shape[2:])
    return jnp.concatenate([parts[:, k] for k in order], axis=1)


def spline(phase):
    rest = 1.0 - phase
    cube = phase * phase * phase
    square = phase * phase
    first = rest * rest * rest / 6.0
    second = (3.0 * cube - 6.0 * square + 4.0) / 6.0
    third = (-3.0 * cube + 3.0 * square + 3.0 * phase + 1.0) / 6.0
    fourth = cube / 6.0
    return (first, second, third, fourth)


def local(
    src_design,
    att_design,
    obs_phase,
    cal_design,
    obs_weight,
    knot_index,
    cal_block,
    cal_column,
    obs_count,
    src_res,
    att_res,
    cal_res,
    src_dir,
    att_dir,
    cal_dir,
):
    knot_count = att_dir.shape[1]
    blocks, col_width = cal_dir.shape
    all_blocks = blocks * lax.axis_size("cal")
    cal_size = all_blocks * col_width
    lane = 128
    rows = cal_size // lane
    src_rows, slots = obs_phase.shape

    cal_values = doubling_gather(cal_dir[None], "cal")[0]
    first_row = (lax.axis_index("tm") == 0).astype(jnp.float32)
    edge_knots = passed_along(att_dir[:, :3], ("tm", "cal"), -1)
    att_ext = jnp.concatenate([att_dir, edge_knots], axis=1)

    live_mask = (lax.broadcasted_iota(jnp.int32, obs_phase.shape, 1) < obs_count[:, None]).astype(
        jnp.float32
    )
    basis = spline(obs_phase)
    local_knot = knot_index - lax.axis_index(("tm", "cal")) * knot_count

    n_obs = src_rows * slots
    flat = lambda a: a.reshape(1, n_obs)

    knot_hot = (flat(local_knot) == lax.broadcasted_iota(jnp.int32, (knot_count, 1), 0)).astype(jnp.float32)

    table = jnp.stack([att_ext[:, m : m + knot_count] for m in range(4)], axis=0).reshape(12, knot_count)
    picked = jnp.dot(table, knot_hot, precision=ONE_HOT_PRECISION).reshape(4, 3, src_rows, slots)
    y_att = jnp.zeros_like(obs_phase)
    for m in range(4):
        y_att = y_att + basis[m] * jnp.sum(att_design * picked[m], axis=0)

    flat_index = flat(cal_block * col_width + cal_column)
    high_hot = (flat_index // lane == lax.broadcasted_iota(jnp.int32, (rows, 1), 0)).astype(jnp.float32)
    low_hot = (flat_index % lane == lax.broadcasted_iota(jnp.int32, (lane, 1), 0)).astype(jnp.float32)
    cal_table = cal_values.reshape(rows, lane)
    row_vals = lax.dot_general(cal_table, high_hot, (((0,), (0,)), ((), ())), precision=ONE_HOT_PRECISION)
    y_cal = cal_design * jnp.sum(row_vals * low_hot, axis=0).reshape(src_rows, slots)

    y_src = jnp.sum(src_design * src_dir[:, :, None], axis=0)
    response = live_mask * (y_src + y_att + y_cal)
    weighted = obs_weight * response
    curv_local = jnp.sum(weighted * response)
    q_src = jnp.sum(src_design * weighted[None], axis=2)

    scaled = att_design * weighted[None]
    spread = jnp.stack([basis[m][None] * scaled for m in range(4)], axis=0).reshape(12, n_obs)
    gathered = lax.dot_general(spread, knot_hot, (((1,), (1,)), ((), ())), precision=ONE_HOT_PRECISION)
    gathered = gathered.reshape(4, 3, knot_count)
    grad_ext = jnp.zeros((3, knot_count + 3), jnp.float32)
    for m in range(4):
        grad_ext = grad_ext + jnp.pad(gathered[m], ((0, 0), (m, 3 - m)))
    incoming = passed_along(grad_ext[:, knot_count:], ("tm", "cal"), 1)
    q_att = jnp.concatenate([grad_ext[:, :3] + incoming, grad_ext[:, 3:knot_count]], axis=1)

    cal_weighted = flat(cal_design * weighted) * low_hot
    cal_term = lax.dot_general(high_hot, cal_weighted, (((1,), (1,)), ((), ())), precision=ONE_HOT_PRECISION)
    res_sq = jnp.sum(src_res * src_res) + jnp.sum(att_res * att_res)
    cal_sq = first_row * jnp.sum(cal_res * cal_res)
    res_q = jnp.sum(src_res * q_src) + jnp.sum(att_res * q_att)
    q_sq = jnp.sum(q_src * q_src) + jnp.sum(q_att * q_att)
    scalars = jnp.stack([res_sq, curv_local, res_q, q_sq, cal_sq])
    scalars = jnp.concatenate([scalars, jnp.zeros((lane - 5,), jnp.float32)]).reshape(1, lane)
    own_rows, scalars = halving_sum(cal_term, scalars, "cal")
    summed = jnp.concatenate([own_rows, scalars], axis=0)
    distance = lax.axis_size("tm") // 2
    while distance >= 1:
        summed = summed + exchanged(summed, "tm", distance)
        distance //= 2
    res_sq, curvature, res_q, q_sq, cal_sq = (summed[-1, k] for k in range(5))
    q_cal = summed[:-1].reshape(blocks, col_width)

    norm_now = res_sq + cal_sq
    step_len = norm_now / curvature
    new_src_res = src_res - step_len * q_src
    new_att_res = att_res - step_len * q_att
    new_cal_res = cal_res - step_len * q_cal
    kept = res_sq - step_len * (2.0 * res_q - step_len * q_sq)
    cal_next = jnp.broadcast_to(jnp.sum(new_cal_res * new_cal_res), (1, lane))
    norm_next = kept + doubling_sum(cal_next, "cal")[0, 0]
    ratio = norm_next / norm_now
    return (
        new_src_res,
        new_att_res,
        new_cal_res,
        new_src_res + ratio * src_dir,
        new_att_res + ratio * att_dir,
        new_cal_res + ratio * cal_dir,
    )


def solution(mesh):
    return jax.shard_map(
        local,
        mesh=mesh,
        in_specs=(
            P(None, ("tm", "cal"), None),
            P(None, ("tm", "cal"), None),
            P(("tm", "cal"), None),
            P(("tm", "cal"), None),
            P(("tm", "cal"), None),
            P(("tm", "cal"), None),
            P(("tm", "cal"), None),
            P(("tm", "cal"), None),
            P(("tm", "cal")),
            P(None, ("tm", "cal")),
            P(None, ("tm", "cal")),
            P("cal", None),
            P(None, ("tm", "cal")),
            P(None, ("tm", "cal")),
            P("cal", None),
        ),
        out_specs=(
            P(None, ("tm", "cal")),
            P(None, ("tm", "cal")),
            P("cal", None),
            P(None, ("tm", "cal")),
            P(None, ("tm", "cal")),
            P("cal", None),
        ),
        check_vma=False,
    )
```
